256 devices in a mesh: batch: 8 (over x, core), tensor: 32 (over y, z).
Axes of the slice: x: 4, y: 4, z: 8, core: 2. Of those that a mesh axis runs over, the one named last changes fastest.
Arguments:
- inputs: bfloat16 [4, 8, 32, 4096], P(None, 'batch', 'tensor'), may hold values from -6 to 6
- norm_gain: float32 [4096], replicated, may hold values from 0.5 to 1.5
- norm_bias: float32 [4096], replicated, may hold values from -3 to 3
- qkv_weight: bfloat16 [4096, 3, 4096], P(None, None, 'tensor'), may hold values from -0.09375 to 0.09375
- out_weight: bfloat16 [4096, 4096], P('tensor'), may hold values from -0.375 to 0.375
- in_weight: bfloat16 [4096, 8192], P(None, 'tensor'), may hold values from -0.09375 to 0.09375
- in_bias: float32 [8192], P('tensor'), may hold values from -3 to 3
- down_weight: bfloat16 [8192, 4096], P('tensor'), may hold values from -0.0625 to 0.0625
- down_bias: float32 [4096], replicated, may hold values from -3 to 3
- page_pool: bfloat16 [128, 2, 128, 4096], P('batch', None, None, 'tensor'), may hold values from -103 to 103
- old_cache: bfloat16 [8, 32, 2, 64, 4096], P('batch', None, None, None, 'tensor'), may hold values from -103 to 103, as said below
- page_table: int32 [32, 4], replicated, may hold values from 0 to 127, as said below
- prompt_length: int32 [32], replicated, may hold values from 1 to 512, 8192 in all
- parents: int32 [4, 8, 32], replicated, may hold values from 0 to 7
Outputs:
- outputs: float32 [4, 8, 32, 4096], P(None, 'batch', 'tensor')
The draws below stay inside these ranges and needn't reach their ends.
Inputs may be any that keep to these rules, and one draw needn't show every extreme that they name: `old_cache`: key and value entries of the beams' generated tokens. `page_table`: every pool page is named exactly once in the table. The pool is cut into as many equal blocks of consecutive pages as the batch axis has devices; request r names only pages of block r modulo that count.
All inputs are finite; a program needn't handle non-finite values.
Results may differ from the reference program's by a relative error of at most 0.034.
Values may be sent and summed in bfloat16 or wider, within the bound.
No kernel may reach another device: no remote copies, remote signals or barrier semaphores. Data moves between devices by JAX's collectives and lax.ppermute only.
A program may use at most 128 MiB of HBM per device.

```python
import math
import jax
import jax.numpy as jnp
import numpy as np
from jax import lax

D = 4096
HEADS = 16
HDIM = 256
ROT = 64
FF = 8192
BEAMS = 8
REQ = 32
STEPS = 4
PAGE = 128
PPAGES = 4
GEN = 64
POOL = 128
N_BATCH = 8


def cache_entries(key, array_shape):
    return jnp.clip(jax.random.normal(jax.random.fold_in(key, 13), array_shape, jnp.float32), -4.0, 4.0)


def draw_page_pool(key, part):
    return cache_entries(key, (POOL, 2, PAGE, HEADS * HDIM)).astype(jnp.bfloat16)


def draw_old_cache(key, part):
    return cache_entries(key, (BEAMS, REQ, 2, GEN, HEADS * HDIM)).astype(jnp.bfloat16)


def draw_page_table(key, part):
    group_count = N_BATCH
    pages_each = POOL // group_count
    owned_requests = REQ // group_count
    group_keys = jax.random.split(jax.random.fold_in(key, 21), group_count)
    shuffled = jax.vmap(lambda single: jax.random.permutation(single, pages_each))(group_keys)
    local_table = shuffled.reshape(group_count, owned_requests, PPAGES)
    offsets = (jnp.arange(group_count) * pages_each)[:, None, None]
    placed = local_table + offsets
    return jnp.transpose(placed, (1, 0, 2)).reshape(REQ, PPAGES).astype(jnp.int32)


def set_ends(array, rng, smallest, largest):
    dims = array.shape
    place = [jax.random.randint(jax.random.fold_in(rng, axis), (), 0, dims[axis]) for axis in range(len(dims))]
    array = array.at[tuple(place)].set(smallest)
    longest = dims.index(max(dims))
    place[longest] = (place[longest] + 1) % dims[longest]
    return array.at[tuple(place)].set(largest)


def block_scale(rng, dims, cuts, least, high):
    def one(dim, shards_of):
        heights = jax.random.uniform(jax.random.fold_in(jax.random.fold_in(rng, 6), dim), (shards_of,), jnp.float32, least / len(cuts), high / len(cuts))
        return jnp.repeat(jnp.exp(heights), dims[dim] // shards_of).reshape((-1,) + (1,) * (len(dims) - dim - 1))

    level = one(*cuts[0])
    for cut in cuts[1:]:
        level = level * one(*cut)
    return level


def profile(amount, total, limit, slope):
    portions = [(1 << 20) // math.isqrt(grade ** slope) + 1 for grade in range(2, amount + 1)]
    spare, holding = total - limit - (amount - 1), [1] * (amount - 1)
    while spare > 0:
        candidates = [i for i in range(amount - 1) if holding[i] < limit]
        whole, left = sum([portions[i] for i in candidates]), spare
        for i in candidates:
            addition = min(limit - holding[i], max(1, left * portions[i] // whole), spare)
            holding[i] = holding[i] + addition
            spare = spare - addition
    return np.array([limit] + holding)


def ragged_sizes(key, count, total, limit, skew):
    if count == 2:
        one = jax.random.randint(key, (), max(1, total - limit), min(limit, total - 1) + 1)
        return jnp.stack([one, total - one])
    lengths = jnp.asarray(profile(count, total, limit, skew), jnp.int32)
    couples = (count - 1) // 2
    donor, receiver = lengths[1:1 + 2 * couples:2], lengths[2:2 + 2 * couples:2]
    slack = jnp.minimum(donor - 1, limit - receiver)
    moved = jax.random.randint(jax.random.fold_in(key, 1), (couples,), 0, 1 << 20) % (slack + 1)
    lengths = lengths.at[1:1 + 2 * couples:2].set(donor - moved).at[2:2 + 2 * couples:2].set(receiver + moved)
    return lengths[jax.random.permutation(jax.random.fold_in(key, 2), count)]


def bell_draw(own_key, dims, width, most, cuts=(), held_as=jnp.bfloat16):
    gain = block_scale(own_key, dims, cuts, -0.22, 0.18) if cuts else 1.0
    drawn = jax.random.normal(own_key, dims, jnp.float32) * width * gain
    return jnp.minimum(jnp.maximum(drawn, -most), most).astype(held_as)


def setup_inputs(seed: int = 0) -> dict:
    splits = jax.random.split(jax.random.key(seed), 15)
    return {
        "inputs": bell_draw(splits[0], (STEPS, BEAMS, REQ, D), 1.0, 6.0, ((1, 8), (2, 32))),
        "norm_gain": jnp.clip(1.0 + 0.1 * jax.random.normal(splits[1], (D,), jnp.float32), 0.5, 1.5),
        "norm_bias": bell_draw(splits[2], (D,), 0.5, 3.0, (), jnp.float32),
        "qkv_weight": bell_draw(splits[3], (D, 3, HEADS * HDIM), D ** -0.5, 0.09375, ((2, 32),)),
        "out_weight": bell_draw(splits[4], (HEADS * HDIM, D), HDIM ** -0.5, 0.375, ((0, 32),)),
        "in_weight": bell_draw(splits[5], (D, FF), D ** -0.5, 0.09375, ((1, 32),)),
        "in_bias": bell_draw(splits[6], (FF,), 0.5, 3.0, ((0, 32),), jnp.float32),
        "down_weight": bell_draw(splits[7], (FF, D), FF ** -0.5, 0.0625, ((0, 32),)),
        "down_bias": bell_draw(splits[8], (D,), 0.5, 3.0, (), jnp.float32),
        "page_pool": draw_page_pool(jax.random.fold_in(splits[14], 71), 0),
        "old_cache": draw_old_cache(jax.random.fold_in(splits[14], 71), 0),
        "page_table": draw_page_table(jax.random.fold_in(splits[14], 71), 0),
        "prompt_length": ragged_sizes(splits[12], REQ, REQ * PPAGES * PAGE // 2, PPAGES * PAGE, 2).astype(jnp.int32),
        "parents": set_ends(jax.random.randint(splits[13], (STEPS, BEAMS, REQ), 0, BEAMS), jax.random.fold_in(splits[13], 1), 0, BEAMS - 1).astype(jnp.int32),
    }


def normalize(row_block, norm_gain, norm_bias):
    widened = row_block.astype(jnp.float32)
    center = lax.optimization_barrier(jnp.mean(widened, axis=-1, keepdims=True))
    shifted = widened - center
    variance = lax.optimization_barrier(jnp.mean(shifted * shifted, axis=-1, keepdims=True))
    return shifted * lax.rsqrt(variance + 1e-05) * norm_gain + norm_bias

def rotate_heads(vectors, position):
    halves = vectors.reshape(vectors.shape[:-1] + (HDIM // 2, 2))
    doubled = 2 * jnp.arange(HDIM // 2)
    exponent = doubled.astype(jnp.float32) / ROT
    frequency = jnp.where(doubled < ROT, jnp.exp(-exponent * math.log(10000.0)), 0.0)
    angles = position[:, None] * frequency[None, :]
    cosine = jnp.cos(angles)[None, :, None, :]
    sine_part = jnp.sin(angles)[None, :, None, :]
    even_part = halves[..., 0]
    odd_part = halves[..., 1]
    turned = jnp.stack([even_part * cosine - odd_part * sine_part, odd_part * cosine + even_part * sine_part], axis=-1)
    return turned.reshape(vectors.shape)

def reference(inputs, norm_gain, norm_bias, qkv_weight, out_weight, in_weight, in_bias, down_weight, down_bias, page_pool, old_cache, page_table, prompt_length, parents):
    total_width = HEADS * HDIM
    cache_span = GEN + STEPS
    prompt_span = PPAGES * PAGE
    scale_factor = HDIM ** (-0.5)
    cache = jnp.concatenate([old_cache, jnp.zeros((BEAMS, REQ, 2, STEPS, total_width), jnp.bfloat16)], axis=3)
    prompt_valid = jnp.arange(prompt_span)[None, :] < prompt_length[:, None]
    request_ids = jnp.arange(REQ).astype(jnp.int32)
    outputs = []
    for step_index in range(STEPS):
        current = inputs[step_index]
        normed = normalize(current, norm_gain, norm_bias).astype(jnp.bfloat16)
        flat_rows = normed.reshape(BEAMS * REQ, D)
        projected = jnp.dot(flat_rows, qkv_weight.reshape(D, 3 * total_width), preferred_element_type=jnp.float32)
        projected = projected.reshape(BEAMS, REQ, 3, HEADS, HDIM)
        position = (prompt_length + GEN + step_index).astype(jnp.float32)
        queries = rotate_heads(projected[:, :, 0], position).astype(jnp.bfloat16)
        fresh_keys = rotate_heads(projected[:, :, 1], position).astype(jnp.bfloat16)
        fresh_values = projected[:, :, 2].astype(jnp.bfloat16)
        cache = cache[parents[step_index], request_ids[None, :]]
        new_entry = jnp.stack([fresh_keys.reshape(BEAMS, REQ, total_width), fresh_values.reshape(BEAMS, REQ, total_width)], axis=2)
        cache = cache.at[:, :, :, GEN + step_index].set(new_entry)
        live_mask = jnp.arange(cache_span) <= GEN + step_index

        def attend(request_id):
            query_rows = lax.dynamic_index_in_dim(queries, request_id, 1, keepdims=False).astype(jnp.float32)
            beam_cache = lax.dynamic_index_in_dim(cache, request_id, 1, keepdims=False)
            table_row = lax.dynamic_index_in_dim(page_table, request_id, 0, keepdims=False)
            valid_row = lax.dynamic_index_in_dim(prompt_valid, request_id, 0, keepdims=False)
            page_rows = page_pool[table_row]
            prompt_keys = page_rows[:, 0].reshape(prompt_span, HEADS, HDIM).astype(jnp.float32)
            prompt_values = page_rows[:, 1].reshape(prompt_span, HEADS, HDIM).astype(jnp.float32)
            own_keys = beam_cache[:, 0].reshape(BEAMS, cache_span, HEADS, HDIM).astype(jnp.float32)
            own_values = beam_cache[:, 1].reshape(BEAMS, cache_span, HEADS, HDIM).astype(jnp.float32)
            prompt_scores = jnp.einsum('bhd,thd->bht', query_rows, prompt_keys) * scale_factor
            own_scores = jnp.einsum('bhd,bthd->bht', query_rows, own_keys) * scale_factor
            prompt_scores = jnp.where(valid_row[None, None, :], prompt_scores, -jnp.inf)
            own_scores = jnp.where(live_mask[None, None, :], own_scores, -jnp.inf)
            peak = jnp.maximum(lax.optimization_barrier(jnp.max(prompt_scores, axis=-1)), lax.optimization_barrier(jnp.max(own_scores, axis=-1)))
            prompt_exp = jnp.exp(prompt_scores - peak[..., None])
            own_exp = jnp.exp(own_scores - peak[..., None])
            totals = lax.optimization_barrier(jnp.sum(prompt_exp, axis=-1)) + lax.optimization_barrier(jnp.sum(own_exp, axis=-1))
            prompt_round = lax.optimization_barrier(prompt_exp.astype(jnp.bfloat16)).astype(jnp.float32)
            own_round = lax.optimization_barrier(own_exp.astype(jnp.bfloat16)).astype(jnp.float32)
            mixture = jnp.einsum('bht,thd->bhd', prompt_round, prompt_values) + jnp.einsum('bht,bthd->bhd', own_round, own_values)
            return (mixture / totals[..., None]).reshape(BEAMS, total_width)
        attended = lax.map(attend, request_ids)
        attention = jnp.transpose(attended, (1, 0, 2)).astype(jnp.bfloat16)
        hidden = jax.nn.gelu(jnp.dot(flat_rows, in_weight, preferred_element_type=jnp.float32) + in_bias, approximate=True).astype(jnp.bfloat16)
        attn_update = jnp.dot(attention.reshape(BEAMS * REQ, total_width), out_weight, preferred_element_type=jnp.float32)
        mlp_update = jnp.dot(hidden, down_weight, preferred_element_type=jnp.float32)
        result = current.astype(jnp.float32) + (attn_update + mlp_update).reshape(BEAMS, REQ, D) + down_bias
        outputs.append(result.astype(jnp.float32))
    return jnp.stack(outputs, axis=0)
```

```python
import math

import jax
import jax.numpy as jnp
from jax import lax
from jax.sharding import PartitionSpec as P

HDIM = 256
ROT = 64
BEAMS = 8

NEG_FILL = -1e30


def partner(value, axis, bit):
    return lax.ppermute(value, axis, [(i, i ^ 1 << bit) for i in range(lax.axis_size(axis))])


def normalize(row_block, norm_gain, norm_bias):
    widened = row_block.astype(jnp.float32)
    center = jnp.mean(widened, axis=-1, keepdims=True)
    shifted = widened - center
    variance = jnp.mean(shifted * shifted, axis=-1, keepdims=True)
    return shifted * lax.rsqrt(variance + 1e-05) * norm_gain + norm_bias


def rotate_local(vectors, position, first_column):
    half_count = vectors.shape[-1] // 2
    doubled = (first_column + 2 * jnp.arange(half_count)) % HDIM
    exponent = doubled.astype(jnp.float32) / ROT
    frequency = jnp.where(doubled < ROT, jnp.exp(-exponent * math.log(10000.0)), 0.0)
    angles = position[..., None] * frequency
    cosine = jnp.cos(angles)
    sine_part = jnp.sin(angles)
    halves = vectors.reshape(vectors.shape[:-1] + (half_count, 2))
    even_part = halves[..., 0]
    odd_part = halves[..., 1]
    turned = jnp.stack(
        [even_part * cosine - odd_part * sine_part, odd_part * cosine + even_part * sine_part],
        axis=-1,
    )
    return turned.reshape(vectors.shape)


def on_device(
    inputs,
    norm_gain,
    norm_bias,
    qkv_weight,
    out_weight,
    in_weight,
    in_bias,
    down_weight,
    down_bias,
    page_pool,
    old_cache,
    page_table,
    prompt_length,
    parents,
):
    batch_index = lax.axis_index("batch")
    tensor_index = lax.axis_index("tensor")
    groups = lax.axis_size("batch")
    steps = inputs.shape[0]
    model_width = inputs.shape[3]
    columns = qkv_weight.shape[2]
    requests = page_table.shape[0]
    history = old_cache.shape[3]
    page_count = page_table.shape[1]
    page_size = page_pool.shape[2]
    pool_dev = page_pool.shape[0]
    prompt_span = page_count * page_size
    local_reqs = requests // groups
    scale_factor = HDIM ** (-0.5)
    first_column = tensor_index * columns

    normed = normalize(inputs[:, 0], norm_gain, norm_bias).astype(jnp.bfloat16)
    rows = lax.all_gather(normed, "tensor", axis=1, tiled=True)
    flat = rows.reshape(steps * requests, model_width)
    qkv_flat = qkv_weight.reshape(model_width, 3 * columns)
    projected = jnp.dot(flat, qkv_flat, preferred_element_type=jnp.float32).reshape(
        steps, requests, 3 * columns
    )
    ffn = jnp.dot(flat, in_weight, preferred_element_type=jnp.float32).reshape(
        steps, requests, -1
    )
    hidden = jax.nn.gelu(ffn + in_bias, approximate=True).astype(jnp.bfloat16)

    position = (
        prompt_length[None, :] + history + jnp.arange(steps, dtype=jnp.int32)[:, None]
    ).astype(jnp.float32)
    queries = rotate_local(projected[..., :columns], position, first_column).astype(jnp.bfloat16)
    fresh_keys = rotate_local(
        projected[..., columns : 2 * columns], position, first_column
    ).astype(jnp.bfloat16)
    fresh_values = projected[..., 2 * columns :].astype(jnp.bfloat16)

    query_all = lax.all_gather(queries[:, None], "batch", axis=1, tiled=True)

    beam_ids = jnp.broadcast_to(jnp.arange(BEAMS, dtype=jnp.int32)[:, None], (BEAMS, requests))
    new_ok_steps = []
    old_ok_steps = []
    for step_index in range(steps):
        lineage = beam_ids
        per_t = [None] * steps
        for back_step in range(step_index, -1, -1):
            per_t[back_step] = lineage == batch_index
            lineage = jnp.take_along_axis(parents[back_step], lineage, axis=0)
        for t in range(step_index + 1, steps):
            per_t[t] = jnp.zeros((BEAMS, requests), bool)
        new_ok_steps.append(jnp.stack(per_t, axis=-1))
        old_ok_steps.append(lineage == batch_index)
    new_ok = jnp.stack(new_ok_steps, axis=0)
    old_ok = jnp.stack(old_ok_steps, axis=0)

    old_keys = old_cache[0, :, 0]
    old_values = old_cache[0, :, 1]
    old_scores = jnp.einsum(
        "sbrc,rhc->sbrh", query_all, old_keys, preferred_element_type=jnp.float32
    )
    new_scores = jnp.einsum(
        "sbrc,trc->sbrt", query_all, fresh_keys, preferred_element_type=jnp.float32
    )

    query_local = lax.dynamic_index_in_dim(
        query_all.reshape(steps, BEAMS, local_reqs, groups, columns), batch_index, 3, False
    )
    table_local = lax.dynamic_index_in_dim(
        page_table.reshape(local_reqs, groups, page_count), batch_index, 1, False
    ) - batch_index * pool_dev
    table_local = jnp.clip(table_local, 0, pool_dev - 1)
    length_local = lax.dynamic_index_in_dim(
        prompt_length.reshape(local_reqs, groups), batch_index, 1, False
    )
    pages = page_pool[table_local]
    prompt_keys = pages[:, :, 0].reshape(local_reqs, prompt_span, columns)
    prompt_values = pages[:, :, 1].reshape(local_reqs, prompt_span, columns)
    prompt_scores = jnp.einsum(
        "sbrc,rtc->sbrt", query_local, prompt_keys, preferred_element_type=jnp.float32
    )

    other = partner((old_scores, new_scores, prompt_scores), "tensor", 0)
    old_scores = (old_scores + other[0]) * scale_factor
    new_scores = (new_scores + other[1]) * scale_factor
    prompt_scores = (prompt_scores + other[2]) * scale_factor

    old_mask = old_ok[..., None]
    old_masked = jnp.where(old_mask, old_scores, NEG_FILL)
    new_masked = jnp.where(new_ok, new_scores, NEG_FILL)
    chain_peak = jnp.maximum(jnp.max(old_masked, axis=-1), jnp.max(new_masked, axis=-1))
    old_w = jnp.where(old_mask, jnp.exp(old_masked - chain_peak[..., None]), 0.0)
    new_w = jnp.where(new_ok, jnp.exp(new_masked - chain_peak[..., None]), 0.0)
    chain_total = jnp.sum(old_w, axis=-1) + jnp.sum(new_w, axis=-1)
    chain_mix = jnp.einsum(
        "sbrh,rhc->sbrc", old_w.astype(jnp.bfloat16), old_values, preferred_element_type=jnp.float32
    ) + jnp.einsum(
        "sbrt,trc->sbrc",
        new_w.astype(jnp.bfloat16),
        fresh_values,
        preferred_element_type=jnp.float32,
    )

    prompt_mask = (jnp.arange(prompt_span)[None, :] < length_local[:, None])[None, None]
    prompt_masked = jnp.where(prompt_mask, prompt_scores, NEG_FILL)
    prompt_peak = jnp.max(prompt_masked, axis=-1)
    prompt_w = jnp.where(prompt_mask, jnp.exp(prompt_masked - prompt_peak[..., None]), 0.0)
    prompt_total = jnp.sum(prompt_w, axis=-1)
    prompt_mix = jnp.einsum(
        "sbrt,rtc->sbrc",
        prompt_w.astype(jnp.bfloat16),
        prompt_values,
        preferred_element_type=jnp.float32,
    )

    slot_hit = (jnp.arange(groups) == batch_index)[None, None, None, :]
    def spread(values, fill):
        placed = jnp.where(slot_hit, values[..., None], fill)
        return placed.reshape(values.shape[:2] + (requests,))

    def spread_mix(values):
        placed = jnp.where(slot_hit[..., None], values[:, :, :, None, :], 0.0)
        return placed.reshape(values.shape[:2] + (requests, columns))

    p_peak = spread(prompt_peak, NEG_FILL)
    p_total = spread(prompt_total, 0.0)
    p_mix = spread_mix(prompt_mix)
    peak = jnp.maximum(chain_peak, p_peak)
    f_chain = jnp.exp(chain_peak - peak)
    f_prompt = jnp.exp(p_peak - peak)
    total = chain_total * f_chain + p_total * f_prompt
    mix = chain_mix * f_chain[..., None] + p_mix * f_prompt[..., None]

    packed = jnp.concatenate([mix, peak[..., None], total[..., None]], axis=-1)
    received = lax.all_to_all(packed, "batch", 1, 1, tiled=True)
    r_mix = received[..., :columns]
    r_peak = received[..., columns]
    r_total = received[..., columns + 1]
    g_peak = jnp.max(r_peak, axis=1, keepdims=True)
    factor = jnp.exp(r_peak - g_peak)
    all_total = jnp.sum(r_total * factor, axis=1)
    all_mix = jnp.sum(r_mix * factor[..., None], axis=1)
    attention = (all_mix / all_total[..., None]).astype(jnp.bfloat16)

    update = jnp.einsum(
        "src,cd->rsd", attention, out_weight, preferred_element_type=jnp.float32
    ) + jnp.einsum("srf,fd->rsd", hidden, down_weight, preferred_element_type=jnp.float32)
    summed = lax.psum_scatter(update, "tensor", scatter_dimension=0, tiled=True)
    result = inputs[:, 0].astype(jnp.float32) + jnp.transpose(summed, (1, 0, 2)) + down_bias
    return result[:, None]


def solution(mesh):
    in_specs = (
        P(None, "batch", "tensor", None),
        P(),
        P(),
        P(None, None, "tensor"),
        P("tensor", None),
        P(None, "tensor"),
        P("tensor"),
        P("tensor", None),
        P(),
        P("batch", None, None, "tensor"),
        P("batch", None, None, None, "tensor"),
        P(),
        P(),
        P(),
    )
    out_specs = P(None, "batch", "tensor", None)
    return jax.shard_map(
        on_device, mesh=mesh, in_specs=in_specs, out_specs=out_specs, check_vma=False
    )
```

```python
import math

import jax
import jax.numpy as jnp
from jax import lax
from jax.sharding import PartitionSpec as P

HDIM = 256
ROT = 64
BEAMS = 8

NEG_FILL = -1e30
SCATTER_ORDER = (0, 3, 1, 4, 2)
GATHER_ORDER = (2, 4, 1, 3, 0)


def partner(value, axis, bit):
    return lax.ppermute(value, axis, [(i, i ^ 1 << bit) for i in range(lax.axis_size(axis))])


def tree_reduce_scatter(x, axis, order):
    n = x.shape[0]
    nbits = n.bit_length() - 1
    me = lax.axis_index(axis)
    x = x.reshape((2,) * nbits + x.shape[1:])
    remaining = list(range(nbits - 1, -1, -1))
    for k in order:
        a = remaining.index(k)
        bit = (me >> k) & 1
        keep = lax.dynamic_index_in_dim(x, bit, a, keepdims=False)
        send = lax.dynamic_index_in_dim(x, 1 - bit, a, keepdims=False)
        x = keep + partner(send, axis, k)
        remaining.pop(a)
    return x


def tree_all_gather(x, axis, order, out_axis):
    n = lax.axis_size(axis)
    nbits = n.bit_length() - 1
    me = lax.axis_index(axis)
    have = []
    for k in order:
        bit = (me >> k) & 1
        got = partner(x, axis, k)
        low = jnp.where(bit == 0, x, got)
        high = jnp.where(bit == 0, got, x)
        x = jnp.stack([low, high], axis=0)
        have.insert(0, k)
    rest = list(range(nbits, x.ndim))
    lead = [have.index(b) for b in range(nbits - 1, -1, -1)]
    perm = rest[:out_axis] + lead + rest[out_axis:]
    x = jnp.transpose(x, perm)
    return x.reshape(x.shape[:out_axis] + (n,) + x.shape[out_axis + nbits :])


def normalize(row_block, norm_gain, norm_bias):
    widened = row_block.astype(jnp.float32)
    center = jnp.mean(widened, axis=-1, keepdims=True)
    shifted = widened - center
    variance = jnp.mean(shifted * shifted, axis=-1, keepdims=True)
    return shifted * lax.rsqrt(variance + 1e-05) * norm_gain + norm_bias


def rotate_local(vectors, position, first_column):
    half_count = vectors.shape[-1] // 2
    doubled = (first_column + 2 * jnp.arange(half_count)) % HDIM
    exponent = doubled.astype(jnp.float32) / ROT
    frequency = jnp.where(doubled < ROT, jnp.exp(-exponent * math.log(10000.0)), 0.0)
    angles = position[..., None] * frequency
    cosine = jnp.cos(angles)
    sine_part = jnp.sin(angles)
    halves = vectors.reshape(vectors.shape[:-1] + (half_count, 2))
    even_part = halves[..., 0]
    odd_part = halves[..., 1]
    turned = jnp.stack(
        [even_part * cosine - odd_part * sine_part, odd_part * cosine + even_part * sine_part],
        axis=-1,
    )
    return turned.reshape(vectors.shape)


def on_device(
    inputs,
    norm_gain,
    norm_bias,
    qkv_weight,
    out_weight,
    in_weight,
    in_bias,
    down_weight,
    down_bias,
    page_pool,
    old_cache,
    page_table,
    prompt_length,
    parents,
):
    batch_index = lax.axis_index("batch")
    tensor_index = lax.axis_index("tensor")
    groups = lax.axis_size("batch")
    steps = inputs.shape[0]
    model_width = inputs.shape[3]
    columns = qkv_weight.shape[2]
    requests = page_table.shape[0]
    history = old_cache.shape[3]
    page_count = page_table.shape[1]
    page_size = page_pool.shape[2]
    pool_dev = page_pool.shape[0]
    prompt_span = page_count * page_size
    local_reqs = requests // groups
    scale_factor = HDIM ** (-0.5)
    first_column = tensor_index * columns

    normed = normalize(inputs[:, 0], norm_gain, norm_bias).astype(jnp.bfloat16)
    rows = tree_all_gather(normed[:, 0], "tensor", GATHER_ORDER, 1)
    flat = rows.reshape(steps * requests, model_width)
    qkv_flat = qkv_weight.reshape(model_width, 3 * columns)
    projected = jnp.dot(flat, qkv_flat, preferred_element_type=jnp.float32).reshape(
        steps, requests, 3 * columns
    )
    ffn = jnp.dot(flat, in_weight, preferred_element_type=jnp.float32).reshape(
        steps, requests, -1
    )
    hidden = jax.nn.gelu(ffn + in_bias, approximate=True).astype(jnp.bfloat16)

    position = (
        prompt_length[None, :] + history + jnp.arange(steps, dtype=jnp.int32)[:, None]
    ).astype(jnp.float32)
    queries = rotate_local(projected[..., :columns], position, first_column).astype(jnp.bfloat16)
    fresh_keys = rotate_local(
        projected[..., columns : 2 * columns], position, first_column
    ).astype(jnp.bfloat16)
    fresh_values = projected[..., 2 * columns :].astype(jnp.bfloat16)

    query_all = lax.all_gather(queries[:, None], "batch", axis=1, tiled=True)

    beam_ids = jnp.broadcast_to(jnp.arange(BEAMS, dtype=jnp.int32)[:, None], (BEAMS, requests))
    new_ok_steps = []
    old_ok_steps = []
    for step_index in range(steps):
        lineage = beam_ids
        per_t = [None] * steps
        for back_step in range(step_index, -1, -1):
            per_t[back_step] = lineage == batch_index
            pick = lineage[:, None, :] == jnp.arange(BEAMS, dtype=jnp.int32)[None, :, None]
            lineage = jnp.sum(jnp.where(pick, parents[back_step][None], 0), axis=1)
        for t in range(step_index + 1, steps):
            per_t[t] = jnp.zeros((BEAMS, requests), bool)
        new_ok_steps.append(jnp.stack(per_t, axis=-1))
        old_ok_steps.append(lineage == batch_index)
    new_ok = jnp.stack(new_ok_steps, axis=0)
    old_ok = jnp.stack(old_ok_steps, axis=0)

    old_keys = old_cache[0, :, 0]
    old_values = old_cache[0, :, 1]
    old_scores = jnp.einsum(
        "sbrc,rhc->sbrh", query_all, old_keys, preferred_element_type=jnp.float32
    )
    new_scores = jnp.einsum(
        "sbrc,trc->sbrt", query_all, fresh_keys, preferred_element_type=jnp.float32
    )

    query_local = lax.dynamic_index_in_dim(
        query_all.reshape(steps, BEAMS, local_reqs, groups, columns), batch_index, 3, False
    )
    table_local = lax.dynamic_index_in_dim(
        page_table.reshape(local_reqs, groups, page_count), batch_index, 1, False
    ) - batch_index * pool_dev
    table_local = jnp.clip(table_local, 0, pool_dev - 1)
    length_local = lax.dynamic_index_in_dim(
        prompt_length.reshape(local_reqs, groups), batch_index, 1, False
    )
    pages = page_pool[table_local]
    prompt_keys = pages[:, :, 0].reshape(local_reqs, prompt_span, columns)
    prompt_values = pages[:, :, 1].reshape(local_reqs, prompt_span, columns)
    prompt_scores = jnp.einsum(
        "sbrc,rtc->sbrt", query_local, prompt_keys, preferred_element_type=jnp.float32
    )

    other = partner((old_scores, new_scores, prompt_scores), "tensor", 0)
    old_scores = (old_scores + other[0]) * scale_factor
    new_scores = (new_scores + other[1]) * scale_factor
    prompt_scores = (prompt_scores + other[2]) * scale_factor

    old_mask = old_ok[..., None]
    old_masked = jnp.where(old_mask, old_scores, NEG_FILL)
    new_masked = jnp.where(new_ok, new_scores, NEG_FILL)
    chain_peak = jnp.maximum(jnp.max(old_masked, axis=-1), jnp.max(new_masked, axis=-1))
    old_w = jnp.where(old_mask, jnp.exp(old_masked - chain_peak[..., None]), 0.0)
    new_w = jnp.where(new_ok, jnp.exp(new_masked - chain_peak[..., None]), 0.0)
    chain_total = jnp.sum(old_w, axis=-1) + jnp.sum(new_w, axis=-1)
    chain_mix = jnp.einsum(
        "sbrh,rhc->sbrc", old_w.astype(jnp.bfloat16), old_values, preferred_element_type=jnp.float32
    ) + jnp.einsum(
        "sbrt,trc->sbrc",
        new_w.astype(jnp.bfloat16),
        fresh_values,
        preferred_element_type=jnp.float32,
    )

    prompt_mask = (jnp.arange(prompt_span)[None, :] < length_local[:, None])[None, None]
    prompt_masked = jnp.where(prompt_mask, prompt_scores, NEG_FILL)
    prompt_peak = jnp.max(prompt_masked, axis=-1)
    prompt_w = jnp.where(prompt_mask, jnp.exp(prompt_masked - prompt_peak[..., None]), 0.0)
    prompt_total = jnp.sum(prompt_w, axis=-1)
    prompt_mix = jnp.einsum(
        "sbrt,rtc->sbrc",
        prompt_w.astype(jnp.bfloat16),
        prompt_values,
        preferred_element_type=jnp.float32,
    )

    slot_hit = (jnp.arange(groups) == batch_index)[None, None, None, :]
    def spread(values, fill):
        placed = jnp.where(slot_hit, values[..., None], fill)
        return placed.reshape(values.shape[:2] + (requests,))

    def spread_mix(values):
        placed = jnp.where(slot_hit[..., None], values[:, :, :, None, :], 0.0)
        return placed.reshape(values.shape[:2] + (requests, columns))

    p_peak = spread(prompt_peak, NEG_FILL)
    p_total = spread(prompt_total, 0.0)
    p_mix = spread_mix(prompt_mix)
    peak = jnp.maximum(chain_peak, p_peak)
    f_chain = jnp.exp(chain_peak - peak)
    f_prompt = jnp.exp(p_peak - peak)
    total = chain_total * f_chain + p_total * f_prompt
    mix = chain_mix * f_chain[..., None] + p_mix * f_prompt[..., None]

    packed = jnp.concatenate([mix, peak[..., None], total[..., None]], axis=-1)
    received = lax.all_to_all(packed, "batch", 1, 1, tiled=True)
    r_mix = received[..., :columns]
    r_peak = received[..., columns]
    r_total = received[..., columns + 1]
    g_peak = jnp.max(r_peak, axis=1, keepdims=True)
    factor = jnp.exp(r_peak - g_peak)
    all_total = jnp.sum(r_total * factor, axis=1)
    all_mix = jnp.sum(r_mix * factor[..., None], axis=1)
    attention = (all_mix / all_total[..., None]).astype(jnp.bfloat16)

    update = jnp.einsum(
        "src,cd->rsd", attention, out_weight, preferred_element_type=jnp.float32
    ) + jnp.einsum("srf,fd->rsd", hidden, down_weight, preferred_element_type=jnp.float32)
    summed = tree_reduce_scatter(update, "tensor", SCATTER_ORDER)
    result = inputs[:, 0].astype(jnp.float32) + summed[:, None] + down_bias
    return result[:, None]


def solution(mesh):
    in_specs = (
        P(None, "batch", "tensor", None),
        P(),
        P(),
        P(None, None, "tensor"),
        P("tensor", None),
        P(None, "tensor"),
        P("tensor"),
        P("tensor", None),
        P(),
        P("batch", None, None, "tensor"),
        P("batch", None, None, None, "tensor"),
        P(),
        P(),
        P(),
    )
    out_specs = P(None, "batch", "tensor", None)
    return jax.shard_map(
        on_device, mesh=mesh, in_specs=in_specs, out_specs=out_specs, check_vma=False
    )
```

```python
import math

import jax
import jax.numpy as jnp
from jax import lax
from jax.sharding import PartitionSpec as P

HDIM = 256
ROT = 64
BEAMS = 8

NEG_FILL = -1e30
SCATTER_ORDERS = ((0, 3, 1, 4, 2), (3, 0, 4, 1, 2))
GATHER_ORDERS = ((2, 4, 1, 3, 0), (2, 1, 4, 0, 3))


def partner(value, axis, bit):
    return lax.ppermute(value, axis, [(i, i ^ 1 << bit) for i in range(lax.axis_size(axis))])


def tree_reduce_scatter(x, axis, order):
    n = x.shape[0]
    nbits = n.bit_length() - 1
    me = lax.axis_index(axis)
    x = x.reshape((2,) * nbits + x.shape[1:])
    remaining = list(range(nbits - 1, -1, -1))
    for k in order:
        a = remaining.index(k)
        bit = (me >> k) & 1
        keep = lax.dynamic_index_in_dim(x, bit, a, keepdims=False)
        send = lax.dynamic_index_in_dim(x, 1 - bit, a, keepdims=False)
        x = keep + partner(send, axis, k)
        remaining.pop(a)
    return x


def tree_all_gather(x, axis, order, out_axis):
    n = lax.axis_size(axis)
    nbits = n.bit_length() - 1
    me = lax.axis_index(axis)
    have = []
    for k in order:
        bit = (me >> k) & 1
        got = partner(x, axis, k)
        low = jnp.where(bit == 0, x, got)
        high = jnp.where(bit == 0, got, x)
        x = jnp.stack([low, high], axis=0)
        have.insert(0, k)
    rest = list(range(nbits, x.ndim))
    lead = [have.index(b) for b in range(nbits - 1, -1, -1)]
    perm = rest[:out_axis] + lead + rest[out_axis:]
    x = jnp.transpose(x, perm)
    return x.reshape(x.shape[:out_axis] + (n,) + x.shape[out_axis + nbits :])


def split_last(x, count):
    width = x.shape[-1] // count
    return [x[..., i * width : (i + 1) * width] for i in range(count)]


def normalize(row_block, norm_gain, norm_bias):
    widened = row_block.astype(jnp.float32)
    center = jnp.mean(widened, axis=-1, keepdims=True)
    shifted = widened - center
    variance = jnp.mean(shifted * shifted, axis=-1, keepdims=True)
    return shifted * lax.rsqrt(variance + 1e-05) * norm_gain + norm_bias


def rotate_local(vectors, position, first_column):
    half_count = vectors.shape[-1] // 2
    doubled = (first_column + 2 * jnp.arange(half_count)) % HDIM
    exponent = doubled.astype(jnp.float32) / ROT
    frequency = jnp.where(doubled < ROT, jnp.exp(-exponent * math.log(10000.0)), 0.0)
    angles = position[..., None] * frequency
    cosine = jnp.cos(angles)
    sine_part = jnp.sin(angles)
    halves = vectors.reshape(vectors.shape[:-1] + (half_count, 2))
    even_part = halves[..., 0]
    odd_part = halves[..., 1]
    turned = jnp.stack(
        [even_part * cosine - odd_part * sine_part, odd_part * cosine + even_part * sine_part],
        axis=-1,
    )
    return turned.reshape(vectors.shape)


def on_device(
    inputs,
    norm_gain,
    norm_bias,
    qkv_weight,
    out_weight,
    in_weight,
    in_bias,
    down_weight,
    down_bias,
    page_pool,
    old_cache,
    page_table,
    prompt_length,
    parents,
):
    batch_index = lax.axis_index("batch")
    tensor_index = lax.axis_index("tensor")
    groups = lax.axis_size("batch")
    steps = inputs.shape[0]
    model_width = inputs.shape[3]
    columns = qkv_weight.shape[2]
    requests = page_table.shape[0]
    history = old_cache.shape[3]
    page_count = page_table.shape[1]
    page_size = page_pool.shape[2]
    pool_dev = page_pool.shape[0]
    prompt_span = page_count * page_size
    local_reqs = requests // groups
    scale_factor = HDIM ** (-0.5)
    first_column = tensor_index * columns

    normed = normalize(inputs[:, 0], norm_gain, norm_bias).astype(jnp.bfloat16)
    rows = jnp.concatenate(
        [
            tree_all_gather(piece, "tensor", order, 1)
            for piece, order in zip(split_last(normed[:, 0], len(GATHER_ORDERS)), GATHER_ORDERS)
        ],
        axis=-1,
    )
    flat = rows.reshape(steps * requests, model_width)
    qkv_flat = qkv_weight.reshape(model_width, 3 * columns)
    projected = jnp.dot(flat, qkv_flat, preferred_element_type=jnp.float32).reshape(
        steps, requests, 3 * columns
    )
    ffn = jnp.dot(flat, in_weight, preferred_element_type=jnp.float32).reshape(
        steps, requests, -1
    )
    hidden = jax.nn.gelu(ffn + in_bias, approximate=True).astype(jnp.bfloat16)

    position = (
        prompt_length[None, :] + history + jnp.arange(steps, dtype=jnp.int32)[:, None]
    ).astype(jnp.float32)
    queries = rotate_local(projected[..., :columns], position, first_column).astype(jnp.bfloat16)
    fresh_keys = rotate_local(
        projected[..., columns : 2 * columns], position, first_column
    ).astype(jnp.bfloat16)
    fresh_values = projected[..., 2 * columns :].astype(jnp.bfloat16)

    query_all = lax.all_gather(queries[:, None], "batch", axis=1, tiled=True)

    beam_ids = jnp.broadcast_to(jnp.arange(BEAMS, dtype=jnp.int32)[:, None], (BEAMS, requests))
    new_ok_steps = []
    old_ok_steps = []
    for step_index in range(steps):
        lineage = beam_ids
        per_t = [None] * steps
        for back_step in range(step_index, -1, -1):
            per_t[back_step] = lineage == batch_index
            pick = lineage[:, None, :] == jnp.arange(BEAMS, dtype=jnp.int32)[None, :, None]
            lineage = jnp.sum(jnp.where(pick, parents[back_step][None], 0), axis=1)
        for t in range(step_index + 1, steps):
            per_t[t] = jnp.zeros((BEAMS, requests), bool)
        new_ok_steps.append(jnp.stack(per_t, axis=-1))
        old_ok_steps.append(lineage == batch_index)
    new_ok = jnp.stack(new_ok_steps, axis=0)
    old_ok = jnp.stack(old_ok_steps, axis=0)

    old_keys = old_cache[0, :, 0]
    old_values = old_cache[0, :, 1]
    old_scores = jnp.einsum(
        "sbrc,rhc->sbrh", query_all, old_keys, preferred_element_type=jnp.float32
    )
    new_scores = jnp.einsum(
        "sbrc,trc->sbrt", query_all, fresh_keys, preferred_element_type=jnp.float32
    )

    query_local = lax.dynamic_index_in_dim(
        query_all.reshape(steps, BEAMS, local_reqs, groups, columns), batch_index, 3, False
    )
    table_local = lax.dynamic_index_in_dim(
        page_table.reshape(local_reqs, groups, page_count), batch_index, 1, False
    ) - batch_index * pool_dev
    table_local = jnp.clip(table_local, 0, pool_dev - 1)
    length_local = lax.dynamic_index_in_dim(
        prompt_length.reshape(local_reqs, groups), batch_index, 1, False
    )
    pages = page_pool[table_local]
    prompt_keys = pages[:, :, 0].reshape(local_reqs, prompt_span, columns)
    prompt_values = pages[:, :, 1].reshape(local_reqs, prompt_span, columns)
    prompt_scores = jnp.einsum(
        "sbrc,rtc->sbrt", query_local, prompt_keys, preferred_element_type=jnp.float32
    )

    other = partner((old_scores, new_scores, prompt_scores), "tensor", 0)
    old_scores = (old_scores + other[0]) * scale_factor
    new_scores = (new_scores + other[1]) * scale_factor
    prompt_scores = (prompt_scores + other[2]) * scale_factor

    old_mask = old_ok[..., None]
    old_masked = jnp.where(old_mask, old_scores, NEG_FILL)
    new_masked = jnp.where(new_ok, new_scores, NEG_FILL)
    chain_peak = jnp.maximum(jnp.max(old_masked, axis=-1), jnp.max(new_masked, axis=-1))
    old_w = jnp.where(old_mask, jnp.exp(old_masked - chain_peak[..., None]), 0.0)
    new_w = jnp.where(new_ok, jnp.exp(new_masked - chain_peak[..., None]), 0.0)
    chain_total = jnp.sum(old_w, axis=-1) + jnp.sum(new_w, axis=-1)
    chain_mix = jnp.einsum(
        "sbrh,rhc->sbrc", old_w.astype(jnp.bfloat16), old_values, preferred_element_type=jnp.float32
    ) + jnp.einsum(
        "sbrt,trc->sbrc",
        new_w.astype(jnp.bfloat16),
        fresh_values,
        preferred_element_type=jnp.float32,
    )

    prompt_mask = (jnp.arange(prompt_span)[None, :] < length_local[:, None])[None, None]
    prompt_masked = jnp.where(prompt_mask, prompt_scores, NEG_FILL)
    prompt_peak = jnp.max(prompt_masked, axis=-1)
    prompt_w = jnp.where(prompt_mask, jnp.exp(prompt_masked - prompt_peak[..., None]), 0.0)
    prompt_total = jnp.sum(prompt_w, axis=-1)
    prompt_mix = jnp.einsum(
        "sbrt,rtc->sbrc",
        prompt_w.astype(jnp.bfloat16),
        prompt_values,
        preferred_element_type=jnp.float32,
    )

    slot_hit = (jnp.arange(groups) == batch_index)[None, None, None, :]
    def spread(values, fill):
        placed = jnp.where(slot_hit, values[..., None], fill)
        return placed.reshape(values.shape[:2] + (requests,))

    def spread_mix(values):
        placed = jnp.where(slot_hit[..., None], values[:, :, :, None, :], 0.0)
        return placed.reshape(values.shape[:2] + (requests, columns))

    p_peak = spread(prompt_peak, NEG_FILL)
    p_total = spread(prompt_total, 0.0)
    p_mix = spread_mix(prompt_mix)
    peak = jnp.maximum(chain_peak, p_peak)
    f_chain = jnp.exp(chain_peak - peak)
    f_prompt = jnp.exp(p_peak - peak)
    total = chain_total * f_chain + p_total * f_prompt
    mix = chain_mix * f_chain[..., None] + p_mix * f_prompt[..., None]

    packed = jnp.concatenate([mix, peak[..., None], total[..., None]], axis=-1)
    received = lax.all_to_all(packed, "batch", 1, 1, tiled=True)
    r_mix = received[..., :columns]
    r_peak = received[..., columns]
    r_total = received[..., columns + 1]
    g_peak = jnp.max(r_peak, axis=1, keepdims=True)
    factor = jnp.exp(r_peak - g_peak)
    all_total = jnp.sum(r_total * factor, axis=1)
    all_mix = jnp.sum(r_mix * factor[..., None], axis=1)
    attention = (all_mix / all_total[..., None]).astype(jnp.bfloat16)

    update = jnp.einsum(
        "src,cd->rsd", attention, out_weight, preferred_element_type=jnp.float32
    ) + jnp.einsum("srf,fd->rsd", hidden, down_weight, preferred_element_type=jnp.float32)
    summed = jnp.concatenate(
        [
            tree_reduce_scatter(piece, "tensor", order)
            for piece, order in zip(split_last(update, len(SCATTER_ORDERS)), SCATTER_ORDERS)
        ],
        axis=-1,
    )
    result = inputs[:, 0].astype(jnp.float32) + summed[:, None] + down_bias
    return result[:, None]


def solution(mesh):
    in_specs = (
        P(None, "batch", "tensor", None),
        P(),
        P(),
        P(None, None, "tensor"),
        P("tensor", None),
        P(None, "tensor"),
        P("tensor"),
        P("tensor", None),
        P(),
        P("batch", None, None, "tensor"),
        P("batch", None, None, None, "tensor"),
        P(),
        P(),
        P(),
    )
    out_specs = P(None, "batch", "tensor", None)
    return jax.shard_map(
        on_device, mesh=mesh, in_specs=in_specs, out_specs=out_specs, check_vma=False
    )
```

```python
import math

import jax
import jax.numpy as jnp
from jax import lax
from jax.sharding import PartitionSpec as P

HDIM = 256
ROT = 64
BEAMS = 8

NEG_FILL = -1e30
LINK_TYPE = jnp.bfloat16
SCATTER_ORDERS = ((0, 3, 1, 4, 2), (3, 0, 4, 1, 2))
GATHER_ORDERS = ((2, 4, 1, 3, 0), (2, 1, 4, 0, 3))


def partner(value, axis, bit):
    return lax.ppermute(value, axis, [(i, i ^ 1 << bit) for i in range(lax.axis_size(axis))])


def tree_reduce_scatter(x, axis, order):
    n = x.shape[0]
    nbits = n.bit_length() - 1
    me = lax.axis_index(axis)
    x = x.reshape((2,) * nbits + x.shape[1:])
    remaining = list(range(nbits - 1, -1, -1))
    for k in order:
        a = remaining.index(k)
        bit = (me >> k) & 1
        keep = lax.dynamic_index_in_dim(x, bit, a, keepdims=False)
        send = lax.dynamic_index_in_dim(x, 1 - bit, a, keepdims=False).astype(LINK_TYPE)
        x = keep + partner(send, axis, k).astype(keep.dtype)
        remaining.pop(a)
    return x


def tree_all_gather(x, axis, order, out_axis):
    n = lax.axis_size(axis)
    nbits = n.bit_length() - 1
    me = lax.axis_index(axis)
    have = []
    for k in order:
        bit = (me >> k) & 1
        got = partner(x, axis, k)
        low = jnp.where(bit == 0, x, got)
        high = jnp.where(bit == 0, got, x)
        x = jnp.stack([low, high], axis=0)
        have.insert(0, k)
    rest = list(range(nbits, x.ndim))
    lead = [have.index(b) for b in range(nbits - 1, -1, -1)]
    perm = rest[:out_axis] + lead + rest[out_axis:]
    x = jnp.transpose(x, perm)
    return x.reshape(x.shape[:out_axis] + (n,) + x.shape[out_axis + nbits :])


def split_last(x, count):
    width = x.shape[-1] // count
    return [x[..., i * width : (i + 1) * width] for i in range(count)]


def normalize(row_block, norm_gain, norm_bias):
    widened = row_block.astype(jnp.float32)
    center = jnp.mean(widened, axis=-1, keepdims=True)
    shifted = widened - center
    variance = jnp.mean(shifted * shifted, axis=-1, keepdims=True)
    return shifted * lax.rsqrt(variance + 1e-05) * norm_gain + norm_bias


def rotate_local(vectors, position, first_column):
    half_count = vectors.shape[-1] // 2
    doubled = (first_column + 2 * jnp.arange(half_count)) % HDIM
    exponent = doubled.astype(jnp.float32) / ROT
    frequency = jnp.where(doubled < ROT, jnp.exp(-exponent * math.log(10000.0)), 0.0)
    angles = position[..., None] * frequency
    cosine = jnp.cos(angles)
    sine_part = jnp.sin(angles)
    halves = vectors.reshape(vectors.shape[:-1] + (half_count, 2))
    even_part = halves[..., 0]
    odd_part = halves[..., 1]
    turned = jnp.stack(
        [even_part * cosine - odd_part * sine_part, odd_part * cosine + even_part * sine_part],
        axis=-1,
    )
    return turned.reshape(vectors.shape)


def on_device(
    inputs,
    norm_gain,
    norm_bias,
    qkv_weight,
    out_weight,
    in_weight,
    in_bias,
    down_weight,
    down_bias,
    page_pool,
    old_cache,
    page_table,
    prompt_length,
    parents,
):
    batch_index = lax.axis_index("batch")
    tensor_index = lax.axis_index("tensor")
    groups = lax.axis_size("batch")
    steps = inputs.shape[0]
    model_width = inputs.shape[3]
    columns = qkv_weight.shape[2]
    requests = page_table.shape[0]
    history = old_cache.shape[3]
    page_count = page_table.shape[1]
    page_size = page_pool.shape[2]
    pool_dev = page_pool.shape[0]
    prompt_span = page_count * page_size
    local_reqs = requests // groups
    scale_factor = HDIM ** (-0.5)
    first_column = tensor_index * columns

    normed = normalize(inputs[:, 0], norm_gain, norm_bias).astype(jnp.bfloat16)
    rows = jnp.concatenate(
        [
            tree_all_gather(piece, "tensor", order, 1)
            for piece, order in zip(split_last(normed[:, 0], len(GATHER_ORDERS)), GATHER_ORDERS)
        ],
        axis=-1,
    )
    flat = rows.reshape(steps * requests, model_width)
    qkv_flat = qkv_weight.reshape(model_width, 3 * columns)
    projected = jnp.dot(flat, qkv_flat, preferred_element_type=jnp.float32).reshape(
        steps, requests, 3 * columns
    )
    ffn = jnp.dot(flat, in_weight, preferred_element_type=jnp.float32).reshape(
        steps, requests, -1
    )
    hidden = jax.nn.gelu(ffn + in_bias, approximate=True).astype(jnp.bfloat16)

    position = (
        prompt_length[None, :] + history + jnp.arange(steps, dtype=jnp.int32)[:, None]
    ).astype(jnp.float32)
    queries = rotate_local(projected[..., :columns], position, first_column).astype(jnp.bfloat16)
    fresh_keys = rotate_local(
        projected[..., columns : 2 * columns], position, first_column
    ).astype(jnp.bfloat16)
    fresh_values = projected[..., 2 * columns :].astype(jnp.bfloat16)

    query_all = lax.all_gather(queries[:, None], "batch", axis=1, tiled=True)

    beam_ids = jnp.broadcast_to(jnp.arange(BEAMS, dtype=jnp.int32)[:, None], (BEAMS, requests))
    new_ok_steps = []
    old_ok_steps = []
    for step_index in range(steps):
        lineage = beam_ids
        per_t = [None] * steps
        for back_step in range(step_index, -1, -1):
            per_t[back_step] = lineage == batch_index
            pick = lineage[:, None, :] == jnp.arange(BEAMS, dtype=jnp.int32)[None, :, None]
            lineage = jnp.sum(jnp.where(pick, parents[back_step][None], 0), axis=1)
        for t in range(step_index + 1, steps):
            per_t[t] = jnp.zeros((BEAMS, requests), bool)
        new_ok_steps.append(jnp.stack(per_t, axis=-1))
        old_ok_steps.append(lineage == batch_index)
    new_ok = jnp.stack(new_ok_steps, axis=0)
    old_ok = jnp.stack(old_ok_steps, axis=0)

    old_keys = old_cache[0, :, 0]
    old_values = old_cache[0, :, 1]
    old_scores = jnp.einsum(
        "sbrc,rhc->sbrh", query_all, old_keys, preferred_element_type=jnp.float32
    )
    new_scores = jnp.einsum(
        "sbrc,trc->sbrt", query_all, fresh_keys, preferred_element_type=jnp.float32
    )

    query_local = lax.dynamic_index_in_dim(
        query_all.reshape(steps, BEAMS, local_reqs, groups, columns), batch_index, 3, False
    )
    table_local = lax.dynamic_index_in_dim(
        page_table.reshape(local_reqs, groups, page_count), batch_index, 1, False
    ) - batch_index * pool_dev
    table_local = jnp.clip(table_local, 0, pool_dev - 1)
    length_local = lax.dynamic_index_in_dim(
        prompt_length.reshape(local_reqs, groups), batch_index, 1, False
    )
    pages = page_pool[table_local]
    prompt_keys = pages[:, :, 0].reshape(local_reqs, prompt_span, columns)
    prompt_values = pages[:, :, 1].reshape(local_reqs, prompt_span, columns)
    prompt_scores = jnp.einsum(
        "sbrc,rtc->sbrt", query_local, prompt_keys, preferred_element_type=jnp.float32
    )

    other = partner((old_scores, new_scores, prompt_scores), "tensor", 0)
    old_scores = (old_scores + other[0]) * scale_factor
    new_scores = (new_scores + other[1]) * scale_factor
    prompt_scores = (prompt_scores + other[2]) * scale_factor

    old_mask = old_ok[..., None]
    old_masked = jnp.where(old_mask, old_scores, NEG_FILL)
    new_masked = jnp.where(new_ok, new_scores, NEG_FILL)
    chain_peak = jnp.maximum(jnp.max(old_masked, axis=-1), jnp.max(new_masked, axis=-1))
    old_w = jnp.where(old_mask, jnp.exp(old_masked - chain_peak[..., None]), 0.0)
    new_w = jnp.where(new_ok, jnp.exp(new_masked - chain_peak[..., None]), 0.0)
    chain_total = jnp.sum(old_w, axis=-1) + jnp.sum(new_w, axis=-1)
    chain_mix = jnp.einsum(
        "sbrh,rhc->sbrc", old_w.astype(jnp.bfloat16), old_values, preferred_element_type=jnp.float32
    ) + jnp.einsum(
        "sbrt,trc->sbrc",
        new_w.astype(jnp.bfloat16),
        fresh_values,
        preferred_element_type=jnp.float32,
    )

    prompt_mask = (jnp.arange(prompt_span)[None, :] < length_local[:, None])[None, None]
    prompt_masked = jnp.where(prompt_mask, prompt_scores, NEG_FILL)
    prompt_peak = jnp.max(prompt_masked, axis=-1)
    prompt_w = jnp.where(prompt_mask, jnp.exp(prompt_masked - prompt_peak[..., None]), 0.0)
    prompt_total = jnp.sum(prompt_w, axis=-1)
    prompt_mix = jnp.einsum(
        "sbrt,rtc->sbrc",
        prompt_w.astype(jnp.bfloat16),
        prompt_values,
        preferred_element_type=jnp.float32,
    )

    slot_hit = (jnp.arange(groups) == batch_index)[None, None, None, :]
    def spread(values, fill):
        placed = jnp.where(slot_hit, values[..., None], fill)
        return placed.reshape(values.shape[:2] + (requests,))

    def spread_mix(values):
        placed = jnp.where(slot_hit[..., None], values[:, :, :, None, :], 0.0)
        return placed.reshape(values.shape[:2] + (requests, columns))

    p_peak = spread(prompt_peak, NEG_FILL)
    p_total = spread(prompt_total, 0.0)
    p_mix = spread_mix(prompt_mix)
    peak = jnp.maximum(chain_peak, p_peak)
    f_chain = jnp.exp(chain_peak - peak)
    f_prompt = jnp.exp(p_peak - peak)
    total = chain_total * f_chain + p_total * f_prompt
    mix = chain_mix * f_chain[..., None] + p_mix * f_prompt[..., None]

    packed = jnp.concatenate([mix, peak[..., None], total[..., None]], axis=-1)
    received = lax.all_to_all(packed, "batch", 1, 1, tiled=True)
    r_mix = received[..., :columns]
    r_peak = received[..., columns]
    r_total = received[..., columns + 1]
    g_peak = jnp.max(r_peak, axis=1, keepdims=True)
    factor = jnp.exp(r_peak - g_peak)
    all_total = jnp.sum(r_total * factor, axis=1)
    all_mix = jnp.sum(r_mix * factor[..., None], axis=1)
    attention = (all_mix / all_total[..., None]).astype(jnp.bfloat16)

    update = jnp.einsum(
        "src,cd->rsd", attention, out_weight, preferred_element_type=jnp.float32
    ) + jnp.einsum("srf,fd->rsd", hidden, down_weight, preferred_element_type=jnp.float32)
    summed = jnp.concatenate(
        [
            tree_reduce_scatter(piece, "tensor", order)
            for piece, order in zip(split_last(update, len(SCATTER_ORDERS)), SCATTER_ORDERS)
        ],
        axis=-1,
    )
    result = inputs[:, 0].astype(jnp.float32) + summed[:, None] + down_bias
    return result[:, None]


def solution(mesh):
    in_specs = (
        P(None, "batch", "tensor", None),
        P(),
        P(),
        P(None, None, "tensor"),
        P("tensor", None),
        P(None, "tensor"),
        P("tensor"),
        P("tensor", None),
        P(),
        P("batch", None, None, "tensor"),
        P("batch", None, None, None, "tensor"),
        P(),
        P(),
        P(),
    )
    out_specs = P(None, "batch", "tensor", None)
    return jax.shard_map(
        on_device, mesh=mesh, in_specs=in_specs, out_specs=out_specs, check_vma=False
    )
```

```python
import math

import jax
import jax.numpy as jnp
from jax import lax
from jax.sharding import PartitionSpec as P

HDIM = 256
ROT = 64
BEAMS = 8

NEG_FILL = -1e30
LINK_TYPE = jnp.bfloat16
SCATTER_ORDERS = ((0, 3, 1, 4, 2), (3, 0, 4, 1, 2))
GATHER_ORDERS = ((2, 4, 1, 3, 0), (2, 1, 4, 0, 3))


def partner(value, axis, bit):
    return lax.ppermute(value, axis, [(i, i ^ 1 << bit) for i in range(lax.axis_size(axis))])


def tree_reduce_scatter(x, axis, order):
    n = x.shape[0]
    nbits = n.bit_length() - 1
    me = lax.axis_index(axis)
    x = x.reshape((2,) * nbits + x.shape[1:])
    remaining = list(range(nbits - 1, -1, -1))
    for k in order:
        a = remaining.index(k)
        bit = (me >> k) & 1
        keep = lax.dynamic_index_in_dim(x, bit, a, keepdims=False)
        send = lax.dynamic_index_in_dim(x, 1 - bit, a, keepdims=False).astype(LINK_TYPE)
        x = keep + partner(send, axis, k).astype(keep.dtype)
        remaining.pop(a)
    return x


def tree_all_gather(x, axis, order, out_axis):
    n = lax.axis_size(axis)
    nbits = n.bit_length() - 1
    me = lax.axis_index(axis)
    have = []
    for k in order:
        bit = (me >> k) & 1
        got = partner(x, axis, k)
        low = jnp.where(bit == 0, x, got)
        high = jnp.where(bit == 0, got, x)
        x = jnp.stack([low, high], axis=0)
        have.insert(0, k)
    rest = list(range(nbits, x.ndim))
    lead = [have.index(b) for b in range(nbits - 1, -1, -1)]
    perm = rest[:out_axis] + lead + rest[out_axis:]
    x = jnp.transpose(x, perm)
    return x.reshape(x.shape[:out_axis] + (n,) + x.shape[out_axis + nbits :])


def split_last(x, count):
    width = x.shape[-1] // count
    return [x[..., i * width : (i + 1) * width] for i in range(count)]


def normalize(row_block, norm_gain, norm_bias):
    widened = row_block.astype(jnp.float32)
    center = jnp.mean(widened, axis=-1, keepdims=True)
    shifted = widened - center
    variance = jnp.mean(shifted * shifted, axis=-1, keepdims=True)
    return shifted * lax.rsqrt(variance + 1e-05) * norm_gain + norm_bias


def rotate_local(vectors, position, first_column):
    half_count = vectors.shape[-1] // 2
    doubled = (first_column + 2 * jnp.arange(half_count)) % HDIM
    exponent = doubled.astype(jnp.float32) / ROT
    frequency = jnp.where(doubled < ROT, jnp.exp(-exponent * math.log(10000.0)), 0.0)
    angles = position[..., None] * frequency
    cosine = jnp.cos(angles)
    sine_part = jnp.sin(angles)
    halves = vectors.reshape(vectors.shape[:-1] + (half_count, 2))
    even_part = halves[..., 0]
    odd_part = halves[..., 1]
    turned = jnp.stack(
        [even_part * cosine - odd_part * sine_part, odd_part * cosine + even_part * sine_part],
        axis=-1,
    )
    return turned.reshape(vectors.shape)


def on_device(
    inputs,
    norm_gain,
    norm_bias,
    qkv_weight,
    out_weight,
    in_weight,
    in_bias,
    down_weight,
    down_bias,
    page_pool,
    old_cache,
    page_table,
    prompt_length,
    parents,
):
    batch_index = lax.axis_index("batch")
    tensor_index = lax.axis_index("tensor")
    groups = lax.axis_size("batch")
    steps = inputs.shape[0]
    model_width = inputs.shape[3]
    columns = qkv_weight.shape[2]
    requests = page_table.shape[0]
    history = old_cache.shape[3]
    page_count = page_table.shape[1]
    page_size = page_pool.shape[2]
    pool_dev = page_pool.shape[0]
    prompt_span = page_count * page_size
    local_reqs = requests // groups
    scale_factor = HDIM ** (-0.5)
    first_column = tensor_index * columns

    table_local = lax.dynamic_index_in_dim(
        page_table.reshape(local_reqs, groups, page_count), batch_index, 1, False
    ) - batch_index * pool_dev
    table_local = jnp.clip(table_local, 0, pool_dev - 1)
    length_local = lax.dynamic_index_in_dim(
        prompt_length.reshape(local_reqs, groups), batch_index, 1, False
    )
    pages = page_pool[table_local]
    prompt_keys = pages[:, :, 0].reshape(local_reqs, prompt_span, columns)
    prompt_values = pages[:, :, 1].reshape(local_reqs, prompt_span, columns)
    old_keys = old_cache[0, :, 0]
    other_old, other_prompt = partner((old_keys, prompt_keys), "tensor", 0)
    old_keys_full = jnp.concatenate([old_keys, other_old], axis=-1)
    prompt_keys_full = jnp.concatenate([prompt_keys, other_prompt], axis=-1)

    normed = normalize(inputs[:, 0], norm_gain, norm_bias).astype(jnp.bfloat16)
    rows = jnp.concatenate(
        [
            tree_all_gather(piece, "tensor", order, 1)
            for piece, order in zip(split_last(normed[:, 0], len(GATHER_ORDERS)), GATHER_ORDERS)
        ],
        axis=-1,
    )
    flat = rows.reshape(steps * requests, model_width)
    qkv_flat = qkv_weight.reshape(model_width, 3 * columns)
    projected = jnp.dot(flat, qkv_flat, preferred_element_type=jnp.float32).reshape(
        steps, requests, 3 * columns
    )
    ffn = jnp.dot(flat, in_weight, preferred_element_type=jnp.float32).reshape(
        steps, requests, -1
    )
    hidden = jax.nn.gelu(ffn + in_bias, approximate=True).astype(jnp.bfloat16)

    position = (
        prompt_length[None, :] + history + jnp.arange(steps, dtype=jnp.int32)[:, None]
    ).astype(jnp.float32)
    queries = rotate_local(projected[..., :columns], position, first_column).astype(jnp.bfloat16)
    fresh_keys = rotate_local(
        projected[..., columns : 2 * columns], position, first_column
    ).astype(jnp.bfloat16)
    fresh_values = projected[..., 2 * columns :].astype(jnp.bfloat16)

    other_q, other_k = partner((queries, fresh_keys), "tensor", 0)
    query_full = jnp.concatenate([queries, other_q], axis=-1)
    fresh_keys_full = jnp.concatenate([fresh_keys, other_k], axis=-1)

    query_all = lax.all_gather(query_full[:, None], "batch", axis=1, tiled=True)

    beam_ids = jnp.broadcast_to(jnp.arange(BEAMS, dtype=jnp.int32)[:, None], (BEAMS, requests))
    new_ok_steps = []
    old_ok_steps = []
    for step_index in range(steps):
        lineage = beam_ids
        per_t = [None] * steps
        for back_step in range(step_index, -1, -1):
            per_t[back_step] = lineage == batch_index
            pick = lineage[:, None, :] == jnp.arange(BEAMS, dtype=jnp.int32)[None, :, None]
            lineage = jnp.sum(jnp.where(pick, parents[back_step][None], 0), axis=1)
        for t in range(step_index + 1, steps):
            per_t[t] = jnp.zeros((BEAMS, requests), bool)
        new_ok_steps.append(jnp.stack(per_t, axis=-1))
        old_ok_steps.append(lineage == batch_index)
    new_ok = jnp.stack(new_ok_steps, axis=0)
    old_ok = jnp.stack(old_ok_steps, axis=0)

    old_values = old_cache[0, :, 1]
    old_scores = jnp.einsum(
        "sbrc,rhc->sbrh", query_all, old_keys_full, preferred_element_type=jnp.float32
    ) * scale_factor
    new_scores = jnp.einsum(
        "sbrc,trc->sbrt", query_all, fresh_keys_full, preferred_element_type=jnp.float32
    ) * scale_factor

    query_local = lax.dynamic_index_in_dim(
        query_all.reshape(steps, BEAMS, local_reqs, groups, 2 * columns), batch_index, 3, False
    )
    prompt_scores = jnp.einsum(
        "sbrc,rtc->sbrt", query_local, prompt_keys_full, preferred_element_type=jnp.float32
    ) * scale_factor

    old_mask = old_ok[..., None]
    old_masked = jnp.where(old_mask, old_scores, NEG_FILL)
    new_masked = jnp.where(new_ok, new_scores, NEG_FILL)
    chain_peak = jnp.maximum(jnp.max(old_masked, axis=-1), jnp.max(new_masked, axis=-1))
    old_w = jnp.where(old_mask, jnp.exp(old_masked - chain_peak[..., None]), 0.0)
    new_w = jnp.where(new_ok, jnp.exp(new_masked - chain_peak[..., None]), 0.0)
    chain_total = jnp.sum(old_w, axis=-1) + jnp.sum(new_w, axis=-1)
    chain_mix = jnp.einsum(
        "sbrh,rhc->sbrc", old_w.astype(jnp.bfloat16), old_values, preferred_element_type=jnp.float32
    ) + jnp.einsum(
        "sbrt,trc->sbrc",
        new_w.astype(jnp.bfloat16),
        fresh_values,
        preferred_element_type=jnp.float32,
    )

    prompt_mask = (jnp.arange(prompt_span)[None, :] < length_local[:, None])[None, None]
    prompt_masked = jnp.where(prompt_mask, prompt_scores, NEG_FILL)
    prompt_peak = jnp.max(prompt_masked, axis=-1)
    prompt_w = jnp.where(prompt_mask, jnp.exp(prompt_masked - prompt_peak[..., None]), 0.0)
    prompt_total = jnp.sum(prompt_w, axis=-1)
    prompt_mix = jnp.einsum(
        "sbrt,rtc->sbrc",
        prompt_w.astype(jnp.bfloat16),
        prompt_values,
        preferred_element_type=jnp.float32,
    )

    slot_hit = (jnp.arange(groups) == batch_index)[None, None, None, :]
    def spread(values, fill):
        placed = jnp.where(slot_hit, values[..., None], fill)
        return placed.reshape(values.shape[:2] + (requests,))

    def spread_mix(values):
        placed = jnp.where(slot_hit[..., None], values[:, :, :, None, :], 0.0)
        return placed.reshape(values.shape[:2] + (requests, columns))

    p_peak = spread(prompt_peak, NEG_FILL)
    p_total = spread(prompt_total, 0.0)
    p_mix = spread_mix(prompt_mix)
    peak = jnp.maximum(chain_peak, p_peak)
    f_chain = jnp.exp(chain_peak - peak)
    f_prompt = jnp.exp(p_peak - peak)
    total = chain_total * f_chain + p_total * f_prompt
    mix = chain_mix * f_chain[..., None] + p_mix * f_prompt[..., None]

    packed = jnp.concatenate([mix, peak[..., None], total[..., None]], axis=-1)
    received = lax.all_to_all(packed, "batch", 1, 1, tiled=True)
    r_mix = received[..., :columns]
    r_peak = received[..., columns]
    r_total = received[..., columns + 1]
    g_peak = jnp.max(r_peak, axis=1, keepdims=True)
    factor = jnp.exp(r_peak - g_peak)
    all_total = jnp.sum(r_total * factor, axis=1)
    all_mix = jnp.sum(r_mix * factor[..., None], axis=1)
    attention = (all_mix / all_total[..., None]).astype(jnp.bfloat16)

    update = jnp.einsum(
        "src,cd->rsd", attention, out_weight, preferred_element_type=jnp.float32
    ) + jnp.einsum("srf,fd->rsd", hidden, down_weight, preferred_element_type=jnp.float32)
    summed = jnp.concatenate(
        [
            tree_reduce_scatter(piece, "tensor", order)
            for piece, order in zip(split_last(update, len(SCATTER_ORDERS)), SCATTER_ORDERS)
        ],
        axis=-1,
    )
    result = inputs[:, 0].astype(jnp.float32) + summed[:, None] + down_bias
    return result[:, None]


def solution(mesh):
    in_specs = (
        P(None, "batch", "tensor", None),
        P(),
        P(),
        P(None, None, "tensor"),
        P("tensor", None),
        P(None, "tensor"),
        P("tensor"),
        P("tensor", None),
        P(),
        P("batch", None, None, "tensor"),
        P("batch", None, None, None, "tensor"),
        P(),
        P(),
        P(),
    )
    out_specs = P(None, "batch", "tensor", None)
    return jax.shard_map(
        on_device, mesh=mesh, in_specs=in_specs, out_specs=out_specs, check_vma=False
    )
```

```python
import math

import jax
import jax.numpy as jnp
from jax import lax
from jax.sharding import PartitionSpec as P

HDIM = 256
ROT = 64
BEAMS = 8

NEG_FILL = -1e30
LINK_TYPE = jnp.bfloat16
SCATTER_ORDERS = ((0, 3, 1, 4, 2), (3, 0, 4, 1, 2))
GATHER_ORDERS = ((2, 4, 1, 3, 0), (2, 1, 4, 0, 3))
BATCH_GATHER_ORDER = (2, 1, 0)
BATCH_SCATTER_ORDER = (0, 1, 2)


def partner(value, axis, bit):
    return lax.ppermute(value, axis, [(i, i ^ 1 << bit) for i in range(lax.axis_size(axis))])


def tree_reduce_scatter(x, axis, order, merge=None):
    n = x.shape[0]
    nbits = n.bit_length() - 1
    me = lax.axis_index(axis)
    x = x.reshape((2,) * nbits + x.shape[1:])
    remaining = list(range(nbits - 1, -1, -1))
    for k in order:
        a = remaining.index(k)
        bit = (me >> k) & 1
        keep = lax.dynamic_index_in_dim(x, bit, a, keepdims=False)
        send = lax.dynamic_index_in_dim(x, 1 - bit, a, keepdims=False)
        if merge is None:
            x = keep + partner(send.astype(LINK_TYPE), axis, k).astype(keep.dtype)
        else:
            x = merge(keep, partner(send, axis, k))
        remaining.pop(a)
    return x


def tree_all_gather(x, axis, order, out_axis):
    n = lax.axis_size(axis)
    nbits = n.bit_length() - 1
    me = lax.axis_index(axis)
    have = []
    for k in order:
        bit = (me >> k) & 1
        got = partner(x, axis, k)
        low = jnp.where(bit == 0, x, got)
        high = jnp.where(bit == 0, got, x)
        x = jnp.stack([low, high], axis=0)
        have.insert(0, k)
    rest = list(range(nbits, x.ndim))
    lead = [have.index(b) for b in range(nbits - 1, -1, -1)]
    perm = rest[:out_axis] + lead + rest[out_axis:]
    x = jnp.transpose(x, perm)
    return x.reshape(x.shape[:out_axis] + (n,) + x.shape[out_axis + nbits :])


def split_last(x, count):
    width = x.shape[-1] // count
    return [x[..., i * width : (i + 1) * width] for i in range(count)]


def normalize(row_block, norm_gain, norm_bias):
    widened = row_block.astype(jnp.float32)
    center = jnp.mean(widened, axis=-1, keepdims=True)
    shifted = widened - center
    variance = jnp.mean(shifted * shifted, axis=-1, keepdims=True)
    return shifted * lax.rsqrt(variance + 1e-05) * norm_gain + norm_bias


def rotate_local(vectors, position, first_column):
    half_count = vectors.shape[-1] // 2
    doubled = (first_column + 2 * jnp.arange(half_count)) % HDIM
    exponent = doubled.astype(jnp.float32) / ROT
    frequency = jnp.where(doubled < ROT, jnp.exp(-exponent * math.log(10000.0)), 0.0)
    angles = position[..., None] * frequency
    cosine = jnp.cos(angles)
    sine_part = jnp.sin(angles)
    halves = vectors.reshape(vectors.shape[:-1] + (half_count, 2))
    even_part = halves[..., 0]
    odd_part = halves[..., 1]
    turned = jnp.stack(
        [even_part * cosine - odd_part * sine_part, odd_part * cosine + even_part * sine_part],
        axis=-1,
    )
    return turned.reshape(vectors.shape)


def on_device(
    inputs,
    norm_gain,
    norm_bias,
    qkv_weight,
    out_weight,
    in_weight,
    in_bias,
    down_weight,
    down_bias,
    page_pool,
    old_cache,
    page_table,
    prompt_length,
    parents,
):
    batch_index = lax.axis_index("batch")
    tensor_index = lax.axis_index("tensor")
    groups = lax.axis_size("batch")
    steps = inputs.shape[0]
    model_width = inputs.shape[3]
    columns = qkv_weight.shape[2]
    requests = page_table.shape[0]
    history = old_cache.shape[3]
    page_count = page_table.shape[1]
    page_size = page_pool.shape[2]
    pool_dev = page_pool.shape[0]
    prompt_span = page_count * page_size
    local_reqs = requests // groups
    scale_factor = HDIM ** (-0.5)
    first_column = tensor_index * columns

    table_local = lax.dynamic_index_in_dim(
        page_table.reshape(local_reqs, groups, page_count), batch_index, 1, False
    ) - batch_index * pool_dev
    table_local = jnp.clip(table_local, 0, pool_dev - 1)
    length_local = lax.dynamic_index_in_dim(
        prompt_length.reshape(local_reqs, groups), batch_index, 1, False
    )
    pages = page_pool[table_local]
    prompt_keys = pages[:, :, 0].reshape(local_reqs, prompt_span, columns)
    prompt_values = pages[:, :, 1].reshape(local_reqs, prompt_span, columns)
    old_keys = old_cache[0, :, 0]
    other_old, other_prompt = partner((old_keys, prompt_keys), "tensor", 0)
    old_keys_full = jnp.concatenate([old_keys, other_old], axis=-1)
    prompt_keys_full = jnp.concatenate([prompt_keys, other_prompt], axis=-1)

    normed = normalize(inputs[:, 0], norm_gain, norm_bias).astype(jnp.bfloat16)
    rows = jnp.concatenate(
        [
            tree_all_gather(piece, "tensor", order, 1)
            for piece, order in zip(split_last(normed[:, 0], len(GATHER_ORDERS)), GATHER_ORDERS)
        ],
        axis=-1,
    )
    flat = rows.reshape(steps * requests, model_width)
    qkv_flat = qkv_weight.reshape(model_width, 3 * columns)
    projected = jnp.dot(flat, qkv_flat, preferred_element_type=jnp.float32).reshape(
        steps, requests, 3 * columns
    )
    ffn = jnp.dot(flat, in_weight, preferred_element_type=jnp.float32).reshape(
        steps, requests, -1
    )
    hidden = jax.nn.gelu(ffn + in_bias, approximate=True).astype(jnp.bfloat16)

    position = (
        prompt_length[None, :] + history + jnp.arange(steps, dtype=jnp.int32)[:, None]
    ).astype(jnp.float32)
    queries = rotate_local(projected[..., :columns], position, first_column).astype(jnp.bfloat16)
    fresh_keys = rotate_local(
        projected[..., columns : 2 * columns], position, first_column
    ).astype(jnp.bfloat16)
    fresh_values = projected[..., 2 * columns :].astype(jnp.bfloat16)

    other_q, other_k = partner((queries, fresh_keys), "tensor", 0)
    query_full = jnp.concatenate([queries, other_q], axis=-1)
    fresh_keys_full = jnp.concatenate([fresh_keys, other_k], axis=-1)

    query_all = tree_all_gather(query_full, "batch", BATCH_GATHER_ORDER, 1)

    beam_ids = jnp.broadcast_to(jnp.arange(BEAMS, dtype=jnp.int32)[:, None], (BEAMS, requests))
    new_ok_steps = []
    old_ok_steps = []
    for step_index in range(steps):
        lineage = beam_ids
        per_t = [None] * steps
        for back_step in range(step_index, -1, -1):
            per_t[back_step] = lineage == batch_index
            pick = lineage[:, None, :] == jnp.arange(BEAMS, dtype=jnp.int32)[None, :, None]
            lineage = jnp.sum(jnp.where(pick, parents[back_step][None], 0), axis=1)
        for t in range(step_index + 1, steps):
            per_t[t] = jnp.zeros((BEAMS, requests), bool)
        new_ok_steps.append(jnp.stack(per_t, axis=-1))
        old_ok_steps.append(lineage == batch_index)
    new_ok = jnp.stack(new_ok_steps, axis=0)
    old_ok = jnp.stack(old_ok_steps, axis=0)

    old_values = old_cache[0, :, 1]
    old_scores = jnp.einsum(
        "sbrc,rhc->sbrh", query_all, old_keys_full, preferred_element_type=jnp.float32
    ) * scale_factor
    new_scores = jnp.einsum(
        "sbrc,trc->sbrt", query_all, fresh_keys_full, preferred_element_type=jnp.float32
    ) * scale_factor

    query_local = lax.dynamic_index_in_dim(
        query_all.reshape(steps, BEAMS, local_reqs, groups, 2 * columns), batch_index, 3, False
    )
    prompt_scores = jnp.einsum(
        "sbrc,rtc->sbrt", query_local, prompt_keys_full, preferred_element_type=jnp.float32
    ) * scale_factor

    old_mask = old_ok[..., None]
    old_masked = jnp.where(old_mask, old_scores, NEG_FILL)
    new_masked = jnp.where(new_ok, new_scores, NEG_FILL)
    chain_peak = jnp.maximum(jnp.max(old_masked, axis=-1), jnp.max(new_masked, axis=-1))
    old_w = jnp.where(old_mask, jnp.exp(old_masked - chain_peak[..., None]), 0.0)
    new_w = jnp.where(new_ok, jnp.exp(new_masked - chain_peak[..., None]), 0.0)
    chain_total = jnp.sum(old_w, axis=-1) + jnp.sum(new_w, axis=-1)
    chain_mix = jnp.einsum(
        "sbrh,rhc->sbrc", old_w.astype(jnp.bfloat16), old_values, preferred_element_type=jnp.float32
    ) + jnp.einsum(
        "sbrt,trc->sbrc",
        new_w.astype(jnp.bfloat16),
        fresh_values,
        preferred_element_type=jnp.float32,
    )

    prompt_mask = (jnp.arange(prompt_span)[None, :] < length_local[:, None])[None, None]
    prompt_masked = jnp.where(prompt_mask, prompt_scores, NEG_FILL)
    prompt_peak = jnp.max(prompt_masked, axis=-1)
    prompt_w = jnp.where(prompt_mask, jnp.exp(prompt_masked - prompt_peak[..., None]), 0.0)
    prompt_total = jnp.sum(prompt_w, axis=-1)
    prompt_mix = jnp.einsum(
        "sbrt,rtc->sbrc",
        prompt_w.astype(jnp.bfloat16),
        prompt_values,
        preferred_element_type=jnp.float32,
    )

    slot_hit = (jnp.arange(groups) == batch_index)[None, None, None, :]
    def spread(values, fill):
        placed = jnp.where(slot_hit, values[..., None], fill)
        return placed.reshape(values.shape[:2] + (requests,))

    def spread_mix(values):
        placed = jnp.where(slot_hit[..., None], values[:, :, :, None, :], 0.0)
        return placed.reshape(values.shape[:2] + (requests, columns))

    p_peak = spread(prompt_peak, NEG_FILL)
    p_total = spread(prompt_total, 0.0)
    p_mix = spread_mix(prompt_mix)
    peak = jnp.maximum(chain_peak, p_peak)
    f_chain = jnp.exp(chain_peak - peak)
    f_prompt = jnp.exp(p_peak - peak)
    total = chain_total * f_chain + p_total * f_prompt
    mix = chain_mix * f_chain[..., None] + p_mix * f_prompt[..., None]

    packed = jnp.concatenate([mix, peak[..., None], total[..., None]], axis=-1)
    packed = jnp.moveaxis(packed, 1, 0)

    def merge(one, two):
        top = jnp.maximum(one[..., columns], two[..., columns])
        f_one = jnp.exp(one[..., columns] - top)[..., None]
        f_two = jnp.exp(two[..., columns] - top)[..., None]
        mixed = one * f_one + two * f_two
        return jnp.concatenate(
            [mixed[..., :columns], top[..., None], mixed[..., columns + 1 :]], axis=-1
        )

    merged = tree_reduce_scatter(packed, "batch", BATCH_SCATTER_ORDER, merge)
    all_mix = merged[..., :columns]
    all_total = merged[..., columns + 1]
    attention = (all_mix / all_total[..., None]).astype(jnp.bfloat16)

    update = jnp.einsum(
        "src,cd->rsd", attention, out_weight, preferred_element_type=jnp.float32
    ) + jnp.einsum("srf,fd->rsd", hidden, down_weight, preferred_element_type=jnp.float32)
    summed = jnp.concatenate(
        [
            tree_reduce_scatter(piece, "tensor", order)
            for piece, order in zip(split_last(update, len(SCATTER_ORDERS)), SCATTER_ORDERS)
        ],
        axis=-1,
    )
    result = inputs[:, 0].astype(jnp.float32) + summed[:, None] + down_bias
    return result[:, None]


def solution(mesh):
    in_specs = (
        P(None, "batch", "tensor", None),
        P(),
        P(),
        P(None, None, "tensor"),
        P("tensor", None),
        P(None, "tensor"),
        P("tensor"),
        P("tensor", None),
        P(),
        P("batch", None, None, "tensor"),
        P("batch", None, None, None, "tensor"),
        P(),
        P(),
        P(),
    )
    out_specs = P(None, "batch", "tensor", None)
    return jax.shard_map(
        on_device, mesh=mesh, in_specs=in_specs, out_specs=out_specs, check_vma=False
    )
```

```python
import math

import jax
import jax.numpy as jnp
from jax import lax
from jax.sharding import PartitionSpec as P

HDIM = 256
ROT = 64
BEAMS = 8

NEG_FILL = -1e30
LINK_TYPE = jnp.bfloat16
SCATTER_ORDERS = ((0, 3, 1, 4, 2), (3, 0, 4, 1, 2))
GATHER_ORDERS = ((2, 4, 1, 3, 0), (2, 1, 4, 0, 3))


def partner(value, axis, bit):
    return lax.ppermute(value, axis, [(i, i ^ 1 << bit) for i in range(lax.axis_size(axis))])


def tree_reduce_scatter(x, axis, order):
    n = x.shape[0]
    nbits = n.bit_length() - 1
    me = lax.axis_index(axis)
    x = x.reshape((2,) * nbits + x.shape[1:])
    remaining = list(range(nbits - 1, -1, -1))
    for k in order:
        a = remaining.index(k)
        bit = (me >> k) & 1
        keep = lax.dynamic_index_in_dim(x, bit, a, keepdims=False)
        send = lax.dynamic_index_in_dim(x, 1 - bit, a, keepdims=False).astype(LINK_TYPE)
        x = keep + partner(send, axis, k).astype(keep.dtype)
        remaining.pop(a)
    return x


def tree_all_gather(x, axis, order, out_axis):
    n = lax.axis_size(axis)
    nbits = n.bit_length() - 1
    me = lax.axis_index(axis)
    have = []
    for k in order:
        bit = (me >> k) & 1
        got = partner(x, axis, k)
        low = jnp.where(bit == 0, x, got)
        high = jnp.where(bit == 0, got, x)
        x = jnp.stack([low, high], axis=0)
        have.insert(0, k)
    rest = list(range(nbits, x.ndim))
    lead = [have.index(b) for b in range(nbits - 1, -1, -1)]
    perm = rest[:out_axis] + lead + rest[out_axis:]
    x = jnp.transpose(x, perm)
    return x.reshape(x.shape[:out_axis] + (n,) + x.shape[out_axis + nbits :])


def split_last(x, count):
    width = x.shape[-1] // count
    return [x[..., i * width : (i + 1) * width] for i in range(count)]


def normalize(row_block, norm_gain, norm_bias):
    widened = row_block.astype(jnp.float32)
    center = jnp.mean(widened, axis=-1, keepdims=True)
    shifted = widened - center
    variance = jnp.mean(shifted * shifted, axis=-1, keepdims=True)
    return shifted * lax.rsqrt(variance + 1e-05) * norm_gain + norm_bias


def rotate_local(vectors, position, first_column):
    half_count = vectors.shape[-1] // 2
    doubled = (first_column + 2 * jnp.arange(half_count)) % HDIM
    exponent = doubled.astype(jnp.float32) / ROT
    frequency = jnp.where(doubled < ROT, jnp.exp(-exponent * math.log(10000.0)), 0.0)
    angles = position[..., None] * frequency
    cosine = jnp.cos(angles)
    sine_part = jnp.sin(angles)
    halves = vectors.reshape(vectors.shape[:-1] + (half_count, 2))
    even_part = halves[..., 0]
    odd_part = halves[..., 1]
    turned = jnp.stack(
        [even_part * cosine - odd_part * sine_part, odd_part * cosine + even_part * sine_part],
        axis=-1,
    )
    return turned.reshape(vectors.shape)


def on_device(
    inputs,
    norm_gain,
    norm_bias,
    qkv_weight,
    out_weight,
    in_weight,
    in_bias,
    down_weight,
    down_bias,
    page_pool,
    old_cache,
    page_table,
    prompt_length,
    parents,
):
    batch_index = lax.axis_index("batch")
    tensor_index = lax.axis_index("tensor")
    groups = lax.axis_size("batch")
    steps = inputs.shape[0]
    model_width = inputs.shape[3]
    columns = qkv_weight.shape[2]
    requests = page_table.shape[0]
    history = old_cache.shape[3]
    page_count = page_table.shape[1]
    page_size = page_pool.shape[2]
    pool_dev = page_pool.shape[0]
    prompt_span = page_count * page_size
    local_reqs = requests // groups
    scale_factor = HDIM ** (-0.5)
    first_column = tensor_index * columns

    table_local = lax.dynamic_index_in_dim(
        page_table.reshape(local_reqs, groups, page_count), batch_index, 1, False
    ) - batch_index * pool_dev
    table_local = jnp.clip(table_local, 0, pool_dev - 1)
    length_local = lax.dynamic_index_in_dim(
        prompt_length.reshape(local_reqs, groups), batch_index, 1, False
    )
    pages = page_pool[table_local]
    prompt_keys = pages[:, :, 0].reshape(local_reqs, prompt_span, columns)
    prompt_values = pages[:, :, 1].reshape(local_reqs, prompt_span, columns)
    old_keys = old_cache[0, :, 0]
    other_old, other_prompt = partner((old_keys, prompt_keys), "tensor", 0)
    old_keys_full = jnp.concatenate([old_keys, other_old], axis=-1)
    prompt_keys_full = jnp.concatenate([prompt_keys, other_prompt], axis=-1)

    normed = normalize(inputs[:, 0], norm_gain, norm_bias).astype(jnp.bfloat16)
    rows = jnp.concatenate(
        [
            tree_all_gather(piece, "tensor", order, 1)
            for piece, order in zip(split_last(normed[:, 0], len(GATHER_ORDERS)), GATHER_ORDERS)
        ],
        axis=-1,
    )
    flat = rows.reshape(steps * requests, model_width)
    qkv_flat = qkv_weight.reshape(model_width, 3 * columns)
    projected = jnp.dot(flat, qkv_flat, preferred_element_type=jnp.float32).reshape(
        steps, requests, 3 * columns
    )
    ffn = jnp.dot(flat, in_weight, preferred_element_type=jnp.float32).reshape(
        steps, requests, -1
    )
    hidden = jax.nn.gelu(ffn + in_bias, approximate=True).astype(jnp.bfloat16)
    ffn_update = lax.optimization_barrier(
        jnp.einsum("srf,fd->rsd", hidden, down_weight, preferred_element_type=jnp.float32)
    )

    position = (
        prompt_length[None, :] + history + jnp.arange(steps, dtype=jnp.int32)[:, None]
    ).astype(jnp.float32)
    queries = rotate_local(projected[..., :columns], position, first_column).astype(jnp.bfloat16)
    fresh_keys = rotate_local(
        projected[..., columns : 2 * columns], position, first_column
    ).astype(jnp.bfloat16)
    fresh_values = projected[..., 2 * columns :].astype(jnp.bfloat16)

    other_q, other_k = partner((queries, fresh_keys), "tensor", 0)
    query_full = jnp.concatenate([queries, other_q], axis=-1)
    fresh_keys_full = jnp.concatenate([fresh_keys, other_k], axis=-1)

    query_all = lax.all_gather(query_full[:, None], "batch", axis=1, tiled=True)

    beam_ids = jnp.broadcast_to(jnp.arange(BEAMS, dtype=jnp.int32)[:, None], (BEAMS, requests))
    choices = jnp.arange(BEAMS, dtype=jnp.int32)[None, :, None]
    new_ok_steps = []
    old_ok_steps = []
    lineage = None
    for step_index in range(steps):
        pick = parents[step_index][:, None, :] == choices
        if lineage is None:
            root = parents[0]
            earlier = None
        else:
            stacked = jnp.concatenate([earlier, root[None]], axis=0)
            moved = jnp.sum(jnp.where(pick[None], stacked[:, None], 0), axis=2)
            earlier, root = moved[:-1], moved[-1]
        own = beam_ids[None]
        earlier = own if earlier is None else jnp.concatenate([earlier, own], axis=0)
        lineage = earlier
        hit = earlier == batch_index
        if step_index + 1 < steps:
            hit = jnp.concatenate(
                [hit, jnp.zeros((steps - 1 - step_index, BEAMS, requests), bool)], axis=0
            )
        new_ok_steps.append(jnp.moveaxis(hit, 0, -1))
        old_ok_steps.append(root == batch_index)
    new_ok = jnp.stack(new_ok_steps, axis=0)
    old_ok = jnp.stack(old_ok_steps, axis=0)

    old_values = old_cache[0, :, 1]
    old_scores = jnp.einsum(
        "sbrc,rhc->sbrh", query_all, old_keys_full, preferred_element_type=jnp.float32
    ) * scale_factor
    new_scores = jnp.einsum(
        "sbrc,trc->sbrt", query_all, fresh_keys_full, preferred_element_type=jnp.float32
    ) * scale_factor

    query_local = lax.dynamic_index_in_dim(
        query_all.reshape(steps, BEAMS, local_reqs, groups, 2 * columns), batch_index, 3, False
    )
    prompt_scores = jnp.einsum(
        "sbrc,rtc->sbrt", query_local, prompt_keys_full, preferred_element_type=jnp.float32
    ) * scale_factor

    old_mask = old_ok[..., None]
    old_masked = jnp.where(old_mask, old_scores, NEG_FILL)
    new_masked = jnp.where(new_ok, new_scores, NEG_FILL)
    chain_peak = jnp.maximum(jnp.max(old_masked, axis=-1), jnp.max(new_masked, axis=-1))
    old_w = jnp.where(old_mask, jnp.exp(old_masked - chain_peak[..., None]), 0.0)
    new_w = jnp.where(new_ok, jnp.exp(new_masked - chain_peak[..., None]), 0.0)
    chain_total = jnp.sum(old_w, axis=-1) + jnp.sum(new_w, axis=-1)
    chain_mix = jnp.einsum(
        "sbrh,rhc->sbrc", old_w.astype(jnp.bfloat16), old_values, preferred_element_type=jnp.float32
    ) + jnp.einsum(
        "sbrt,trc->sbrc",
        new_w.astype(jnp.bfloat16),
        fresh_values,
        preferred_element_type=jnp.float32,
    )

    prompt_mask = (jnp.arange(prompt_span)[None, :] < length_local[:, None])[None, None]
    prompt_masked = jnp.where(prompt_mask, prompt_scores, NEG_FILL)
    prompt_peak = jnp.max(prompt_masked, axis=-1)
    prompt_w = jnp.where(prompt_mask, jnp.exp(prompt_masked - prompt_peak[..., None]), 0.0)
    prompt_total = jnp.sum(prompt_w, axis=-1)
    prompt_mix = jnp.einsum(
        "sbrt,rtc->sbrc",
        prompt_w.astype(jnp.bfloat16),
        prompt_values,
        preferred_element_type=jnp.float32,
    )

    slot_hit = (jnp.arange(groups) == batch_index)[None, None, None, :]
    def spread(values, fill):
        placed = jnp.where(slot_hit, values[..., None], fill)
        return placed.reshape(values.shape[:2] + (requests,))

    def spread_mix(values):
        placed = jnp.where(slot_hit[..., None], values[:, :, :, None, :], 0.0)
        return placed.reshape(values.shape[:2] + (requests, columns))

    p_peak = spread(prompt_peak, NEG_FILL)
    p_total = spread(prompt_total, 0.0)
    p_mix = spread_mix(prompt_mix)
    peak = jnp.maximum(chain_peak, p_peak)
    f_chain = jnp.exp(chain_peak - peak)
    f_prompt = jnp.exp(p_peak - peak)
    total = chain_total * f_chain + p_total * f_prompt
    mix = chain_mix * f_chain[..., None] + p_mix * f_prompt[..., None]

    packed = jnp.concatenate([mix, peak[..., None], total[..., None]], axis=-1)
    received = lax.all_to_all(packed, "batch", 1, 1, tiled=True)
    r_mix = received[..., :columns]
    r_peak = received[..., columns]
    r_total = received[..., columns + 1]
    g_peak = jnp.max(r_peak, axis=1, keepdims=True)
    factor = jnp.exp(r_peak - g_peak)
    all_total = jnp.sum(r_total * factor, axis=1)
    all_mix = jnp.sum(r_mix * factor[..., None], axis=1)
    attention = (all_mix / all_total[..., None]).astype(jnp.bfloat16)

    update = (
        jnp.einsum("src,cd->rsd", attention, out_weight, preferred_element_type=jnp.float32)
        + ffn_update
    )
    summed = jnp.concatenate(
        [
            tree_reduce_scatter(piece, "tensor", order)
            for piece, order in zip(split_last(update, len(SCATTER_ORDERS)), SCATTER_ORDERS)
        ],
        axis=-1,
    )
    result = inputs[:, 0].astype(jnp.float32) + summed[:, None] + down_bias
    return result[:, None]


def solution(mesh):
    in_specs = (
        P(None, "batch", "tensor", None),
        P(),
        P(),
        P(None, None, "tensor"),
        P("tensor", None),
        P(None, "tensor"),
        P("tensor"),
        P("tensor", None),
        P(),
        P("batch", None, None, "tensor"),
        P("batch", None, None, None, "tensor"),
        P(),
        P(),
        P(),
    )
    out_specs = P(None, "batch", "tensor", None)
    return jax.shard_map(
        on_device, mesh=mesh, in_specs=in_specs, out_specs=out_specs, check_vma=False
    )
```

```python
import math

import jax
import jax.numpy as jnp
from jax import lax
from jax.sharding import PartitionSpec as P

HDIM = 256
ROT = 64
BEAMS = 8

NEG_FILL = -1e30
LINK_TYPE = jnp.bfloat16
SCATTER_ORDERS = ((0, 3, 1, 4, 2), (3, 0, 4, 1, 2))
GATHER_ORDERS = ((2, 4, 1, 3, 0), (2, 1, 4, 0, 3))


def partner(value, axis, bit):
    return lax.ppermute(value, axis, [(i, i ^ 1 << bit) for i in range(lax.axis_size(axis))])


def tree_reduce_scatter(x, axis, order):
    n = x.shape[0]
    nbits = n.bit_length() - 1
    me = lax.axis_index(axis)
    x = x.reshape((2,) * nbits + x.shape[1:])
    remaining = list(range(nbits - 1, -1, -1))
    for k in order:
        a = remaining.index(k)
        bit = (me >> k) & 1
        keep = lax.dynamic_index_in_dim(x, bit, a, keepdims=False)
        send = lax.dynamic_index_in_dim(x, 1 - bit, a, keepdims=False).astype(LINK_TYPE)
        x = keep + partner(send, axis, k).astype(keep.dtype)
        remaining.pop(a)
    return x


def tree_all_gather(x, axis, order, out_axis):
    n = lax.axis_size(axis)
    nbits = n.bit_length() - 1
    me = lax.axis_index(axis)
    have = []
    for k in order:
        bit = (me >> k) & 1
        got = partner(x, axis, k)
        low = jnp.where(bit == 0, x, got)
        high = jnp.where(bit == 0, got, x)
        x = jnp.stack([low, high], axis=0)
        have.insert(0, k)
    rest = list(range(nbits, x.ndim))
    lead = [have.index(b) for b in range(nbits - 1, -1, -1)]
    perm = rest[:out_axis] + lead + rest[out_axis:]
    x = jnp.transpose(x, perm)
    return x.reshape(x.shape[:out_axis] + (n,) + x.shape[out_axis + nbits :])


def split_last(x, count):
    width = x.shape[-1] // count
    return [x[..., i * width : (i + 1) * width] for i in range(count)]


def normalize(row_block, norm_gain, norm_bias):
    widened = row_block.astype(jnp.float32)
    center = jnp.mean(widened, axis=-1, keepdims=True)
    shifted = widened - center
    variance = jnp.mean(shifted * shifted, axis=-1, keepdims=True)
    return shifted * lax.rsqrt(variance + 1e-05) * norm_gain + norm_bias


def rotate_local(vectors, position, first_column):
    half_count = vectors.shape[-1] // 2
    doubled = (first_column + 2 * jnp.arange(half_count)) % HDIM
    exponent = doubled.astype(jnp.float32) / ROT
    frequency = jnp.where(doubled < ROT, jnp.exp(-exponent * math.log(10000.0)), 0.0)
    angles = position[..., None] * frequency
    cosine = jnp.cos(angles)
    sine_part = jnp.sin(angles)
    halves = vectors.reshape(vectors.shape[:-1] + (half_count, 2))
    even_part = halves[..., 0]
    odd_part = halves[..., 1]
    turned = jnp.stack(
        [even_part * cosine - odd_part * sine_part, odd_part * cosine + even_part * sine_part],
        axis=-1,
    )
    return turned.reshape(vectors.shape)


def on_device(
    inputs,
    norm_gain,
    norm_bias,
    qkv_weight,
    out_weight,
    in_weight,
    in_bias,
    down_weight,
    down_bias,
    page_pool,
    old_cache,
    page_table,
    prompt_length,
    parents,
):
    batch_index = lax.axis_index("batch")
    tensor_index = lax.axis_index("tensor")
    groups = lax.axis_size("batch")
    steps = inputs.shape[0]
    model_width = inputs.shape[3]
    columns = qkv_weight.shape[2]
    requests = page_table.shape[0]
    history = old_cache.shape[3]
    page_count = page_table.shape[1]
    page_size = page_pool.shape[2]
    pool_dev = page_pool.shape[0]
    prompt_span = page_count * page_size
    local_reqs = requests // groups
    scale_factor = HDIM ** (-0.5)
    first_column = tensor_index * columns

    table_local = lax.dynamic_index_in_dim(
        page_table.reshape(local_reqs, groups, page_count), batch_index, 1, False
    ) - batch_index * pool_dev
    table_local = jnp.clip(table_local, 0, pool_dev - 1)
    length_local = lax.dynamic_index_in_dim(
        prompt_length.reshape(local_reqs, groups), batch_index, 1, False
    )
    pages = page_pool[table_local]
    prompt_keys = pages[:, :, 0].reshape(local_reqs, prompt_span, columns)
    prompt_values = pages[:, :, 1].reshape(local_reqs, prompt_span, columns)
    old_keys = old_cache[0, :, 0]
    other_old, other_prompt = partner((old_keys, prompt_keys), "tensor", 0)
    old_keys_full = jnp.concatenate([old_keys, other_old], axis=-1)
    prompt_keys_full = jnp.concatenate([prompt_keys, other_prompt], axis=-1)

    normed = normalize(inputs[:, 0], norm_gain, norm_bias).astype(jnp.bfloat16)
    rows = jnp.concatenate(
        [
            tree_all_gather(piece, "tensor", order, 1)
            for piece, order in zip(split_last(normed[:, 0], len(GATHER_ORDERS)), GATHER_ORDERS)
        ],
        axis=-1,
    )
    flat = rows.reshape(steps * requests, model_width)
    qkv_flat = qkv_weight.reshape(model_width, 3 * columns)
    projected = jnp.dot(flat, qkv_flat, preferred_element_type=jnp.float32).reshape(
        steps, requests, 3 * columns
    )
    ffn = jnp.dot(flat, in_weight, preferred_element_type=jnp.float32).reshape(
        steps, requests, -1
    )
    hidden = jax.nn.gelu(ffn + in_bias, approximate=True).astype(jnp.bfloat16)
    ffn_update = lax.optimization_barrier(
        jnp.einsum("srf,fd->rsd", hidden, down_weight, preferred_element_type=jnp.float32)
    )

    position = (
        prompt_length[None, :] + history + jnp.arange(steps, dtype=jnp.int32)[:, None]
    ).astype(jnp.float32)
    queries = rotate_local(projected[..., :columns], position, first_column).astype(jnp.bfloat16)
    fresh_keys = rotate_local(
        projected[..., columns : 2 * columns], position, first_column
    ).astype(jnp.bfloat16)
    fresh_values = projected[..., 2 * columns :].astype(jnp.bfloat16)

    other_q, other_k = partner((queries, fresh_keys), "tensor", 0)
    query_full = jnp.concatenate([queries, other_q], axis=-1)
    fresh_keys_full = jnp.concatenate([fresh_keys, other_k], axis=-1)

    query_all = lax.all_gather(query_full[:, None], "batch", axis=1, tiled=True)

    beam_ids = jnp.broadcast_to(jnp.arange(BEAMS, dtype=jnp.int32)[:, None], (BEAMS, requests))
    choices = jnp.arange(BEAMS, dtype=jnp.int32)[None, :, None]
    new_ok_steps = []
    old_ok_steps = []
    lineage = None
    for step_index in range(steps):
        pick = parents[step_index][:, None, :] == choices
        if lineage is None:
            root = parents[0]
            earlier = None
        else:
            stacked = jnp.concatenate([earlier, root[None]], axis=0)
            moved = jnp.sum(jnp.where(pick[None], stacked[:, None], 0), axis=2)
            earlier, root = moved[:-1], moved[-1]
        own = beam_ids[None]
        earlier = own if earlier is None else jnp.concatenate([earlier, own], axis=0)
        lineage = earlier
        hit = earlier == batch_index
        if step_index + 1 < steps:
            hit = jnp.concatenate(
                [hit, jnp.zeros((steps - 1 - step_index, BEAMS, requests), bool)], axis=0
            )
        new_ok_steps.append(jnp.moveaxis(hit, 0, -1))
        old_ok_steps.append(root == batch_index)
    new_ok = jnp.stack(new_ok_steps, axis=0)
    old_ok = jnp.stack(old_ok_steps, axis=0)

    old_values = old_cache[0, :, 1]
    old_scores = jnp.einsum(
        "sbrc,rhc->sbrh", query_all, old_keys_full, preferred_element_type=jnp.float32
    ) * scale_factor
    new_scores = jnp.einsum(
        "sbrc,trc->sbrt", query_all, fresh_keys_full, preferred_element_type=jnp.float32
    ) * scale_factor

    query_local = lax.dynamic_index_in_dim(
        query_all.reshape(steps, BEAMS, local_reqs, groups, 2 * columns), batch_index, 3, False
    )
    prompt_scores = jnp.einsum(
        "sbrc,rtc->sbrt", query_local, prompt_keys_full, preferred_element_type=jnp.float32
    ) * scale_factor

    old_mask = old_ok[..., None]
    old_masked = jnp.where(old_mask, old_scores, NEG_FILL)
    new_masked = jnp.where(new_ok, new_scores, NEG_FILL)
    chain_peak = jnp.maximum(jnp.max(old_masked, axis=-1), jnp.max(new_masked, axis=-1))
    old_w = jnp.where(old_mask, jnp.exp(old_masked - chain_peak[..., None]), 0.0)
    new_w = jnp.where(new_ok, jnp.exp(new_masked - chain_peak[..., None]), 0.0)
    chain_total = jnp.sum(old_w, axis=-1) + jnp.sum(new_w, axis=-1)
    chain_mix = jnp.einsum(
        "sbrh,rhc->sbrc", old_w.astype(jnp.bfloat16), old_values, preferred_element_type=jnp.float32
    ) + jnp.einsum(
        "sbrt,trc->sbrc",
        new_w.astype(jnp.bfloat16),
        fresh_values,
        preferred_element_type=jnp.float32,
    )

    prompt_mask = (jnp.arange(prompt_span)[None, :] < length_local[:, None])[None, None]
    prompt_masked = jnp.where(prompt_mask, prompt_scores, NEG_FILL)
    prompt_peak = jnp.max(prompt_masked, axis=-1)
    prompt_w = jnp.where(prompt_mask, jnp.exp(prompt_masked - prompt_peak[..., None]), 0.0)
    prompt_total = jnp.sum(prompt_w, axis=-1)
    prompt_mix = jnp.einsum(
        "sbrt,rtc->sbrc",
        prompt_w.astype(jnp.bfloat16),
        prompt_values,
        preferred_element_type=jnp.float32,
    )

    slot_hit = (jnp.arange(groups) == batch_index)[None, None, None, :]
    def spread(values, fill):
        placed = jnp.where(slot_hit, values[..., None], fill)
        return placed.reshape(values.shape[:2] + (requests,))

    def spread_mix(values):
        placed = jnp.where(slot_hit[..., None], values[:, :, :, None, :], 0.0)
        return placed.reshape(values.shape[:2] + (requests, columns))

    p_peak = spread(prompt_peak, NEG_FILL)
    p_total = spread(prompt_total, 0.0)
    p_mix = spread_mix(prompt_mix)
    peak = jnp.maximum(chain_peak, p_peak)
    f_chain = jnp.exp(chain_peak - peak)
    f_prompt = jnp.exp(p_peak - peak)
    total = chain_total * f_chain + p_total * f_prompt
    mix = chain_mix * f_chain[..., None] + p_mix * f_prompt[..., None]

    peak_high = peak.astype(jnp.bfloat16)
    peak_low = (peak - peak_high.astype(jnp.float32)).astype(jnp.bfloat16)
    packed = jnp.concatenate(
        [
            mix.astype(jnp.bfloat16),
            peak_high[..., None],
            peak_low[..., None],
            total.astype(jnp.bfloat16)[..., None],
        ],
        axis=-1,
    )
    received = lax.all_to_all(packed, "batch", 1, 1, tiled=True).astype(jnp.float32)
    r_mix = received[..., :columns]
    r_peak = received[..., columns] + received[..., columns + 1]
    r_total = received[..., columns + 2]
    g_peak = jnp.max(r_peak, axis=1, keepdims=True)
    factor = jnp.exp(r_peak - g_peak)
    all_total = jnp.sum(r_total * factor, axis=1)
    all_mix = jnp.sum(r_mix * factor[..., None], axis=1)
    attention = (all_mix / all_total[..., None]).astype(jnp.bfloat16)

    update = (
        jnp.einsum("src,cd->rsd", attention, out_weight, preferred_element_type=jnp.float32)
        + ffn_update
    )
    summed = jnp.concatenate(
        [
            tree_reduce_scatter(piece, "tensor", order)
            for piece, order in zip(split_last(update, len(SCATTER_ORDERS)), SCATTER_ORDERS)
        ],
        axis=-1,
    )
    result = inputs[:, 0].astype(jnp.float32) + summed[:, None] + down_bias
    return result[:, None]


def solution(mesh):
    in_specs = (
        P(None, "batch", "tensor", None),
        P(),
        P(),
        P(None, None, "tensor"),
        P("tensor", None),
        P(None, "tensor"),
        P("tensor"),
        P("tensor", None),
        P(),
        P("batch", None, None, "tensor"),
        P("batch", None, None, None, "tensor"),
        P(),
        P(),
        P(),
    )
    out_specs = P(None, "batch", "tensor", None)
    return jax.shard_map(
        on_device, mesh=mesh, in_specs=in_specs, out_specs=out_specs, check_vma=False
    )
```

```python
import math

import jax
import jax.numpy as jnp
from jax import lax
from jax.sharding import PartitionSpec as P

HDIM = 256
ROT = 64
BEAMS = 8

NEG_FILL = -1e30
LINK_TYPE = jnp.bfloat16
SCATTER_ORDERS = ((0, 3, 1, 4, 2), (3, 0, 4, 1, 2))
GATHER_ORDERS = ((2, 4, 1, 3, 0), (2, 1, 4, 0, 3))


def partner(value, axis, bit):
    return lax.ppermute(value, axis, [(i, i ^ 1 << bit) for i in range(lax.axis_size(axis))])


def tree_reduce_scatter(x, axis, order):
    n = x.shape[0]
    nbits = n.bit_length() - 1
    me = lax.axis_index(axis)
    x = x.reshape((2,) * nbits + x.shape[1:])
    remaining = list(range(nbits - 1, -1, -1))
    for k in order:
        a = remaining.index(k)
        bit = (me >> k) & 1
        keep = lax.dynamic_index_in_dim(x, bit, a, keepdims=False)
        send = lax.dynamic_index_in_dim(x, 1 - bit, a, keepdims=False).astype(LINK_TYPE)
        x = keep + partner(send, axis, k).astype(keep.dtype)
        remaining.pop(a)
    return x


def tree_all_gather(x, axis, order, out_axis):
    n = lax.axis_size(axis)
    nbits = n.bit_length() - 1
    me = lax.axis_index(axis)
    have = []
    for k in order:
        bit = (me >> k) & 1
        got = partner(x, axis, k)
        low = jnp.where(bit == 0, x, got)
        high = jnp.where(bit == 0, got, x)
        x = jnp.stack([low, high], axis=0)
        have.insert(0, k)
    rest = list(range(nbits, x.ndim))
    lead = [have.index(b) for b in range(nbits - 1, -1, -1)]
    perm = rest[:out_axis] + lead + rest[out_axis:]
    x = jnp.transpose(x, perm)
    return x.reshape(x.shape[:out_axis] + (n,) + x.shape[out_axis + nbits :])


def split_last(x, count):
    width = x.shape[-1] // count
    return [x[..., i * width : (i + 1) * width] for i in range(count)]


def normalize(row_block, norm_gain, norm_bias):
    widened = row_block.astype(jnp.float32)
    center = jnp.mean(widened, axis=-1, keepdims=True)
    shifted = widened - center
    variance = jnp.mean(shifted * shifted, axis=-1, keepdims=True)
    return shifted * lax.rsqrt(variance + 1e-05) * norm_gain + norm_bias


def rotate_local(vectors, position, first_column):
    half_count = vectors.shape[-1] // 2
    doubled = (first_column + 2 * jnp.arange(half_count)) % HDIM
    exponent = doubled.astype(jnp.float32) / ROT
    frequency = jnp.where(doubled < ROT, jnp.exp(-exponent * math.log(10000.0)), 0.0)
    angles = position[..., None] * frequency
    cosine = jnp.cos(angles)
    sine_part = jnp.sin(angles)
    halves = vectors.reshape(vectors.shape[:-1] + (half_count, 2))
    even_part = halves[..., 0]
    odd_part = halves[..., 1]
    turned = jnp.stack(
        [even_part * cosine - odd_part * sine_part, odd_part * cosine + even_part * sine_part],
        axis=-1,
    )
    return turned.reshape(vectors.shape)


def on_device(
    inputs,
    norm_gain,
    norm_bias,
    qkv_weight,
    out_weight,
    in_weight,
    in_bias,
    down_weight,
    down_bias,
    page_pool,
    old_cache,
    page_table,
    prompt_length,
    parents,
):
    batch_index = lax.axis_index("batch")
    tensor_index = lax.axis_index("tensor")
    groups = lax.axis_size("batch")
    steps = inputs.shape[0]
    model_width = inputs.shape[3]
    columns = qkv_weight.shape[2]
    requests = page_table.shape[0]
    history = old_cache.shape[3]
    page_count = page_table.shape[1]
    page_size = page_pool.shape[2]
    pool_dev = page_pool.shape[0]
    prompt_span = page_count * page_size
    local_reqs = requests // groups
    scale_factor = HDIM ** (-0.5)
    first_column = tensor_index * columns

    table_local = lax.dynamic_index_in_dim(
        page_table.reshape(local_reqs, groups, page_count), batch_index, 1, False
    ) - batch_index * pool_dev
    table_local = jnp.clip(table_local, 0, pool_dev - 1)
    length_local = lax.dynamic_index_in_dim(
        prompt_length.reshape(local_reqs, groups), batch_index, 1, False
    )
    pages = page_pool[table_local]
    prompt_keys = pages[:, :, 0].reshape(local_reqs, prompt_span, columns)
    prompt_values = pages[:, :, 1].reshape(local_reqs, prompt_span, columns)
    old_keys = old_cache[0, :, 0]
    other_old = partner(old_keys, "tensor", 0)
    old_keys_full = jnp.concatenate([old_keys, other_old], axis=-1)

    normed = normalize(inputs[:, 0], norm_gain, norm_bias).astype(jnp.bfloat16)
    rows = jnp.concatenate(
        [
            tree_all_gather(piece, "tensor", order, 1)
            for piece, order in zip(split_last(normed[:, 0], len(GATHER_ORDERS)), GATHER_ORDERS)
        ],
        axis=-1,
    )
    flat = rows.reshape(steps * requests, model_width)
    qkv_flat = qkv_weight.reshape(model_width, 3 * columns)
    projected = jnp.dot(flat, qkv_flat, preferred_element_type=jnp.float32).reshape(
        steps, requests, 3 * columns
    )
    ffn = jnp.dot(flat, in_weight, preferred_element_type=jnp.float32).reshape(
        steps, requests, -1
    )
    hidden = jax.nn.gelu(ffn + in_bias, approximate=True).astype(jnp.bfloat16)
    ffn_update = lax.optimization_barrier(
        jnp.einsum("srf,fd->rsd", hidden, down_weight, preferred_element_type=jnp.float32)
    )

    position = (
        prompt_length[None, :] + history + jnp.arange(steps, dtype=jnp.int32)[:, None]
    ).astype(jnp.float32)
    queries = rotate_local(projected[..., :columns], position, first_column).astype(jnp.bfloat16)
    fresh_keys = rotate_local(
        projected[..., columns : 2 * columns], position, first_column
    ).astype(jnp.bfloat16)
    fresh_values = projected[..., 2 * columns :].astype(jnp.bfloat16)

    other_q, other_k = partner((queries, fresh_keys), "tensor", 0)
    query_full = jnp.concatenate([queries, other_q], axis=-1)
    prompt_keys_late, _ = lax.optimization_barrier((prompt_keys, other_q))
    other_prompt = partner(prompt_keys_late, "tensor", 0)
    prompt_keys_full = jnp.concatenate([prompt_keys, other_prompt], axis=-1)
    fresh_keys_full = jnp.concatenate([fresh_keys, other_k], axis=-1)

    query_all = lax.all_gather(query_full[:, None], "batch", axis=1, tiled=True)

    beam_ids = jnp.broadcast_to(jnp.arange(BEAMS, dtype=jnp.int32)[:, None], (BEAMS, requests))
    choices = jnp.arange(BEAMS, dtype=jnp.int32)[None, :, None]
    new_ok_steps = []
    old_ok_steps = []
    lineage = None
    for step_index in range(steps):
        pick = parents[step_index][:, None, :] == choices
        if lineage is None:
            root = parents[0]
            earlier = None
        else:
            stacked = jnp.concatenate([earlier, root[None]], axis=0)
            moved = jnp.sum(jnp.where(pick[None], stacked[:, None], 0), axis=2)
            earlier, root = moved[:-1], moved[-1]
        own = beam_ids[None]
        earlier = own if earlier is None else jnp.concatenate([earlier, own], axis=0)
        lineage = earlier
        hit = earlier == batch_index
        if step_index + 1 < steps:
            hit = jnp.concatenate(
                [hit, jnp.zeros((steps - 1 - step_index, BEAMS, requests), bool)], axis=0
            )
        new_ok_steps.append(jnp.moveaxis(hit, 0, -1))
        old_ok_steps.append(root == batch_index)
    new_ok = jnp.stack(new_ok_steps, axis=0)
    old_ok = jnp.stack(old_ok_steps, axis=0)

    old_values = old_cache[0, :, 1]
    old_scores = jnp.einsum(
        "sbrc,rhc->sbrh", query_all, old_keys_full, preferred_element_type=jnp.float32
    ) * scale_factor
    new_scores = jnp.einsum(
        "sbrc,trc->sbrt", query_all, fresh_keys_full, preferred_element_type=jnp.float32
    ) * scale_factor

    query_local = lax.dynamic_index_in_dim(
        query_all.reshape(steps, BEAMS, local_reqs, groups, 2 * columns), batch_index, 3, False
    )
    prompt_scores = jnp.einsum(
        "sbrc,rtc->sbrt", query_local, prompt_keys_full, preferred_element_type=jnp.float32
    ) * scale_factor

    old_mask = old_ok[..., None]
    old_masked = jnp.where(old_mask, old_scores, NEG_FILL)
    new_masked = jnp.where(new_ok, new_scores, NEG_FILL)
    chain_peak = jnp.maximum(jnp.max(old_masked, axis=-1), jnp.max(new_masked, axis=-1))
    old_w = jnp.where(old_mask, jnp.exp(old_masked - chain_peak[..., None]), 0.0)
    new_w = jnp.where(new_ok, jnp.exp(new_masked - chain_peak[..., None]), 0.0)
    chain_total = jnp.sum(old_w, axis=-1) + jnp.sum(new_w, axis=-1)
    chain_mix = jnp.einsum(
        "sbrh,rhc->sbrc", old_w.astype(jnp.bfloat16), old_values, preferred_element_type=jnp.float32
    ) + jnp.einsum(
        "sbrt,trc->sbrc",
        new_w.astype(jnp.bfloat16),
        fresh_values,
        preferred_element_type=jnp.float32,
    )

    prompt_mask = (jnp.arange(prompt_span)[None, :] < length_local[:, None])[None, None]
    prompt_masked = jnp.where(prompt_mask, prompt_scores, NEG_FILL)
    prompt_peak = jnp.max(prompt_masked, axis=-1)
    prompt_w = jnp.where(prompt_mask, jnp.exp(prompt_masked - prompt_peak[..., None]), 0.0)
    prompt_total = jnp.sum(prompt_w, axis=-1)
    prompt_mix = jnp.einsum(
        "sbrt,rtc->sbrc",
        prompt_w.astype(jnp.bfloat16),
        prompt_values,
        preferred_element_type=jnp.float32,
    )

    slot_hit = (jnp.arange(groups) == batch_index)[None, None, None, :]
    def spread(values, fill):
        placed = jnp.where(slot_hit, values[..., None], fill)
        return placed.reshape(values.shape[:2] + (requests,))

    def spread_mix(values):
        placed = jnp.where(slot_hit[..., None], values[:, :, :, None, :], 0.0)
        return placed.reshape(values.shape[:2] + (requests, columns))

    p_peak = spread(prompt_peak, NEG_FILL)
    p_total = spread(prompt_total, 0.0)
    p_mix = spread_mix(prompt_mix)
    peak = jnp.maximum(chain_peak, p_peak)
    f_chain = jnp.exp(chain_peak - peak)
    f_prompt = jnp.exp(p_peak - peak)
    total = chain_total * f_chain + p_total * f_prompt
    mix = chain_mix * f_chain[..., None] + p_mix * f_prompt[..., None]

    packed = jnp.concatenate([mix, peak[..., None], total[..., None]], axis=-1)
    received = lax.all_to_all(packed, "batch", 1, 1, tiled=True)
    r_mix = received[..., :columns]
    r_peak = received[..., columns]
    r_total = received[..., columns + 1]
    g_peak = jnp.max(r_peak, axis=1, keepdims=True)
    factor = jnp.exp(r_peak - g_peak)
    all_total = jnp.sum(r_total * factor, axis=1)
    all_mix = jnp.sum(r_mix * factor[..., None], axis=1)
    attention = (all_mix / all_total[..., None]).astype(jnp.bfloat16)

    update = (
        jnp.einsum("src,cd->rsd", attention, out_weight, preferred_element_type=jnp.float32)
        + ffn_update
    )
    summed = jnp.concatenate(
        [
            tree_reduce_scatter(piece, "tensor", order)
            for piece, order in zip(split_last(update, len(SCATTER_ORDERS)), SCATTER_ORDERS)
        ],
        axis=-1,
    )
    result = inputs[:, 0].astype(jnp.float32) + summed[:, None] + down_bias
    return result[:, None]


def solution(mesh):
    in_specs = (
        P(None, "batch", "tensor", None),
        P(),
        P(),
        P(None, None, "tensor"),
        P("tensor", None),
        P(None, "tensor"),
        P("tensor"),
        P("tensor", None),
        P(),
        P("batch", None, None, "tensor"),
        P("batch", None, None, None, "tensor"),
        P(),
        P(),
        P(),
    )
    out_specs = P(None, "batch", "tensor", None)
    return jax.shard_map(
        on_device, mesh=mesh, in_specs=in_specs, out_specs=out_specs, check_vma=False
    )
```

```python
import math

import jax
import jax.numpy as jnp
from jax import lax
from jax.sharding import PartitionSpec as P

HDIM = 256
ROT = 64
BEAMS = 8

NEG_FILL = -1e30
LINK_TYPE = jnp.bfloat16
SCATTER_ORDERS = ((0, 3, 1, 4, 2), (3, 0, 4, 1, 2))
GATHER_ORDERS = ((2, 4, 1, 3, 0), (2, 1, 4, 0, 3))


def partner(value, axis, bit):
    return lax.ppermute(value, axis, [(i, i ^ 1 << bit) for i in range(lax.axis_size(axis))])


def tree_reduce_scatter(x, axis, order):
    n = x.shape[0]
    nbits = n.bit_length() - 1
    me = lax.axis_index(axis)
    x = x.reshape((2,) * nbits + x.shape[1:])
    remaining = list(range(nbits - 1, -1, -1))
    for k in order:
        a = remaining.index(k)
        bit = (me >> k) & 1
        keep = lax.dynamic_index_in_dim(x, bit, a, keepdims=False)
        send = lax.dynamic_index_in_dim(x, 1 - bit, a, keepdims=False).astype(LINK_TYPE)
        x = keep + partner(send, axis, k).astype(keep.dtype)
        remaining.pop(a)
    return x


def tree_all_gather(x, axis, order, out_axis):
    n = lax.axis_size(axis)
    nbits = n.bit_length() - 1
    me = lax.axis_index(axis)
    have = []
    for k in order:
        bit = (me >> k) & 1
        got = partner(x, axis, k)
        low = jnp.where(bit == 0, x, got)
        high = jnp.where(bit == 0, got, x)
        x = jnp.stack([low, high], axis=0)
        have.insert(0, k)
    rest = list(range(nbits, x.ndim))
    lead = [have.index(b) for b in range(nbits - 1, -1, -1)]
    perm = rest[:out_axis] + lead + rest[out_axis:]
    x = jnp.transpose(x, perm)
    return x.reshape(x.shape[:out_axis] + (n,) + x.shape[out_axis + nbits :])


def split_last(x, count):
    width = x.shape[-1] // count
    return [x[..., i * width : (i + 1) * width] for i in range(count)]


def normalize(row_block, norm_gain, norm_bias):
    widened = row_block.astype(jnp.float32)
    center = jnp.mean(widened, axis=-1, keepdims=True)
    shifted = widened - center
    variance = jnp.mean(shifted * shifted, axis=-1, keepdims=True)
    return shifted * lax.rsqrt(variance + 1e-05) * norm_gain + norm_bias


def rotate_local(vectors, position, first_column):
    half_count = vectors.shape[-1] // 2
    doubled = (first_column + 2 * jnp.arange(half_count)) % HDIM
    exponent = doubled.astype(jnp.float32) / ROT
    frequency = jnp.where(doubled < ROT, jnp.exp(-exponent * math.log(10000.0)), 0.0)
    angles = position[..., None] * frequency
    cosine = jnp.cos(angles)
    sine_part = jnp.sin(angles)
    halves = vectors.reshape(vectors.shape[:-1] + (half_count, 2))
    even_part = halves[..., 0]
    odd_part = halves[..., 1]
    turned = jnp.stack(
        [even_part * cosine - odd_part * sine_part, odd_part * cosine + even_part * sine_part],
        axis=-1,
    )
    return turned.reshape(vectors.shape)


def on_device(
    inputs,
    norm_gain,
    norm_bias,
    qkv_weight,
    out_weight,
    in_weight,
    in_bias,
    down_weight,
    down_bias,
    page_pool,
    old_cache,
    page_table,
    prompt_length,
    parents,
):
    batch_index = lax.axis_index("batch")
    tensor_index = lax.axis_index("tensor")
    groups = lax.axis_size("batch")
    steps = inputs.shape[0]
    model_width = inputs.shape[3]
    columns = qkv_weight.shape[2]
    requests = page_table.shape[0]
    history = old_cache.shape[3]
    page_count = page_table.shape[1]
    page_size = page_pool.shape[2]
    pool_dev = page_pool.shape[0]
    prompt_span = page_count * page_size
    local_reqs = requests // groups
    scale_factor = HDIM ** (-0.5)
    first_column = tensor_index * columns

    table_local = lax.dynamic_index_in_dim(
        page_table.reshape(local_reqs, groups, page_count), batch_index, 1, False
    ) - batch_index * pool_dev
    table_local = jnp.clip(table_local, 0, pool_dev - 1)
    length_local = lax.dynamic_index_in_dim(
        prompt_length.reshape(local_reqs, groups), batch_index, 1, False
    )
    pages = page_pool[table_local]
    prompt_keys = pages[:, :, 0].reshape(local_reqs, prompt_span, columns)
    prompt_values = pages[:, :, 1].reshape(local_reqs, prompt_span, columns)
    old_keys = old_cache[0, :, 0]
    other_old, other_prompt = partner((old_keys, prompt_keys), "tensor", 0)
    old_keys_full = jnp.concatenate([old_keys, other_old], axis=-1)
    prompt_keys_full = jnp.concatenate([prompt_keys, other_prompt], axis=-1)

    normed = normalize(inputs[:, 0], norm_gain, norm_bias).astype(jnp.bfloat16)
    rows = jnp.concatenate(
        [
            tree_all_gather(piece, "tensor", order, 1)
            for piece, order in zip(split_last(normed[:, 0], len(GATHER_ORDERS)), GATHER_ORDERS)
        ],
        axis=-1,
    )
    flat = rows.reshape(steps * requests, model_width)
    qkv_flat = qkv_weight.reshape(model_width, 3 * columns)
    projected = jnp.dot(flat, qkv_flat, preferred_element_type=jnp.float32).reshape(
        steps, requests, 3 * columns
    )
    ffn = jnp.dot(flat, in_weight, preferred_element_type=jnp.float32).reshape(
        steps, requests, -1
    )
    hidden = jax.nn.gelu(ffn + in_bias, approximate=True).astype(jnp.bfloat16)
    ffn_update = lax.optimization_barrier(
        [
            jnp.einsum("srf,fd->rsd", hidden, piece, preferred_element_type=jnp.float32)
            for piece in split_last(down_weight, len(SCATTER_ORDERS))
        ]
    )

    position = (
        prompt_length[None, :] + history + jnp.arange(steps, dtype=jnp.int32)[:, None]
    ).astype(jnp.float32)
    queries = rotate_local(projected[..., :columns], position, first_column).astype(jnp.bfloat16)
    fresh_keys = rotate_local(
        projected[..., columns : 2 * columns], position, first_column
    ).astype(jnp.bfloat16)
    fresh_values = projected[..., 2 * columns :].astype(jnp.bfloat16)

    other_q, other_k = partner((queries, fresh_keys), "tensor", 0)
    query_full = jnp.concatenate([queries, other_q], axis=-1)
    fresh_keys_full = jnp.concatenate([fresh_keys, other_k], axis=-1)

    query_all = lax.all_gather(query_full[:, None], "batch", axis=1, tiled=True)

    beam_ids = jnp.broadcast_to(jnp.arange(BEAMS, dtype=jnp.int32)[:, None], (BEAMS, requests))
    choices = jnp.arange(BEAMS, dtype=jnp.int32)[None, :, None]
    new_ok_steps = []
    old_ok_steps = []
    lineage = None
    for step_index in range(steps):
        pick = parents[step_index][:, None, :] == choices
        if lineage is None:
            root = parents[0]
            earlier = None
        else:
            stacked = jnp.concatenate([earlier, root[None]], axis=0)
            moved = jnp.sum(jnp.where(pick[None], stacked[:, None], 0), axis=2)
            earlier, root = moved[:-1], moved[-1]
        own = beam_ids[None]
        earlier = own if earlier is None else jnp.concatenate([earlier, own], axis=0)
        lineage = earlier
        hit = earlier == batch_index
        if step_index + 1 < steps:
            hit = jnp.concatenate(
                [hit, jnp.zeros((steps - 1 - step_index, BEAMS, requests), bool)], axis=0
            )
        new_ok_steps.append(jnp.moveaxis(hit, 0, -1))
        old_ok_steps.append(root == batch_index)
    new_ok = jnp.stack(new_ok_steps, axis=0)
    old_ok = jnp.stack(old_ok_steps, axis=0)

    old_values = old_cache[0, :, 1]
    old_scores = jnp.einsum(
        "sbrc,rhc->sbrh", query_all, old_keys_full, preferred_element_type=jnp.float32
    ) * scale_factor
    new_scores = jnp.einsum(
        "sbrc,trc->sbrt", query_all, fresh_keys_full, preferred_element_type=jnp.float32
    ) * scale_factor

    query_local = lax.dynamic_index_in_dim(
        query_all.reshape(steps, BEAMS, local_reqs, groups, 2 * columns), batch_index, 3, False
    )
    prompt_scores = jnp.einsum(
        "sbrc,rtc->sbrt", query_local, prompt_keys_full, preferred_element_type=jnp.float32
    ) * scale_factor

    old_mask = old_ok[..., None]
    old_masked = jnp.where(old_mask, old_scores, NEG_FILL)
    new_masked = jnp.where(new_ok, new_scores, NEG_FILL)
    chain_peak = jnp.maximum(jnp.max(old_masked, axis=-1), jnp.max(new_masked, axis=-1))
    old_w = jnp.where(old_mask, jnp.exp(old_masked - chain_peak[..., None]), 0.0)
    new_w = jnp.where(new_ok, jnp.exp(new_masked - chain_peak[..., None]), 0.0)
    chain_total = jnp.sum(old_w, axis=-1) + jnp.sum(new_w, axis=-1)
    chain_mix = jnp.einsum(
        "sbrh,rhc->sbrc", old_w.astype(jnp.bfloat16), old_values, preferred_element_type=jnp.float32
    ) + jnp.einsum(
        "sbrt,trc->sbrc",
        new_w.astype(jnp.bfloat16),
        fresh_values,
        preferred_element_type=jnp.float32,
    )

    prompt_mask = (jnp.arange(prompt_span)[None, :] < length_local[:, None])[None, None]
    prompt_masked = jnp.where(prompt_mask, prompt_scores, NEG_FILL)
    prompt_peak = jnp.max(prompt_masked, axis=-1)
    prompt_w = jnp.where(prompt_mask, jnp.exp(prompt_masked - prompt_peak[..., None]), 0.0)
    prompt_total = jnp.sum(prompt_w, axis=-1)
    prompt_mix = jnp.einsum(
        "sbrt,rtc->sbrc",
        prompt_w.astype(jnp.bfloat16),
        prompt_values,
        preferred_element_type=jnp.float32,
    )

    slot_hit = (jnp.arange(groups) == batch_index)[None, None, None, :]
    def spread(values, fill):
        placed = jnp.where(slot_hit, values[..., None], fill)
        return placed.reshape(values.shape[:2] + (requests,))

    def spread_mix(values):
        placed = jnp.where(slot_hit[..., None], values[:, :, :, None, :], 0.0)
        return placed.reshape(values.shape[:2] + (requests, columns))

    p_peak = spread(prompt_peak, NEG_FILL)
    p_total = spread(prompt_total, 0.0)
    p_mix = spread_mix(prompt_mix)
    peak = jnp.maximum(chain_peak, p_peak)
    f_chain = jnp.exp(chain_peak - peak)
    f_prompt = jnp.exp(p_peak - peak)
    total = chain_total * f_chain + p_total * f_prompt
    mix = chain_mix * f_chain[..., None] + p_mix * f_prompt[..., None]

    packed = jnp.concatenate([mix, peak[..., None], total[..., None]], axis=-1)
    received = lax.all_to_all(packed, "batch", 1, 1, tiled=True)
    r_mix = received[..., :columns]
    r_peak = received[..., columns]
    r_total = received[..., columns + 1]
    g_peak = jnp.max(r_peak, axis=1, keepdims=True)
    factor = jnp.exp(r_peak - g_peak)
    all_total = jnp.sum(r_total * factor, axis=1)
    all_mix = jnp.sum(r_mix * factor[..., None], axis=1)
    attention = (all_mix / all_total[..., None]).astype(jnp.bfloat16)

    update = [
        jnp.einsum("src,cd->rsd", attention, piece, preferred_element_type=jnp.float32) + ffn_piece
        for piece, ffn_piece in zip(split_last(out_weight, len(SCATTER_ORDERS)), ffn_update)
    ]
    summed = jnp.concatenate(
        [tree_reduce_scatter(piece, "tensor", order) for piece, order in zip(update, SCATTER_ORDERS)],
        axis=-1,
    )
    result = inputs[:, 0].astype(jnp.float32) + summed[:, None] + down_bias
    return result[:, None]


def solution(mesh):
    in_specs = (
        P(None, "batch", "tensor", None),
        P(),
        P(),
        P(None, None, "tensor"),
        P("tensor", None),
        P(None, "tensor"),
        P("tensor"),
        P("tensor", None),
        P(),
        P("batch", None, None, "tensor"),
        P("batch", None, None, None, "tensor"),
        P(),
        P(),
        P(),
    )
    out_specs = P(None, "batch", "tensor", None)
    return jax.shard_map(
        on_device, mesh=mesh, in_specs=in_specs, out_specs=out_specs, check_vma=False
    )
```

```python
import math

import jax
import jax.numpy as jnp
from jax import lax
from jax.sharding import PartitionSpec as P

HDIM = 256
ROT = 64
BEAMS = 8

NEG_FILL = -1e30
LINK_TYPE = jnp.bfloat16
SCATTER_ORDERS = ((0, 3, 1, 4, 2), (3, 0, 4, 1, 2))
GATHER_ORDERS = ((4, 3, 2, 1, 0), (3, 4, 2, 1, 0))


def partner(value, axis, bit):
    return lax.ppermute(value, axis, [(i, i ^ 1 << bit) for i in range(lax.axis_size(axis))])


def tree_reduce_scatter(x, axis, order):
    n = x.shape[0]
    nbits = n.bit_length() - 1
    me = lax.axis_index(axis)
    x = x.reshape((2,) * nbits + x.shape[1:])
    remaining = list(range(nbits - 1, -1, -1))
    for k in order:
        a = remaining.index(k)
        bit = (me >> k) & 1
        keep = lax.dynamic_index_in_dim(x, bit, a, keepdims=False)
        send = lax.dynamic_index_in_dim(x, 1 - bit, a, keepdims=False).astype(LINK_TYPE)
        x = keep + partner(send, axis, k).astype(keep.dtype)
        remaining.pop(a)
    return x


def tree_all_gather(x, axis, order, out_axis):
    n = lax.axis_size(axis)
    nbits = n.bit_length() - 1
    me = lax.axis_index(axis)
    have = []
    for k in order:
        bit = (me >> k) & 1
        got = partner(x, axis, k)
        low = jnp.where(bit == 0, x, got)
        high = jnp.where(bit == 0, got, x)
        x = jnp.stack([low, high], axis=0)
        have.insert(0, k)
    rest = list(range(nbits, x.ndim))
    lead = [have.index(b) for b in range(nbits - 1, -1, -1)]
    perm = rest[:out_axis] + lead + rest[out_axis:]
    x = jnp.transpose(x, perm)
    return x.reshape(x.shape[:out_axis] + (n,) + x.shape[out_axis + nbits :])


def split_last(x, count):
    width = x.shape[-1] // count
    return [x[..., i * width : (i + 1) * width] for i in range(count)]


def normalize(row_block, norm_gain, norm_bias):
    widened = row_block.astype(jnp.float32)
    center = jnp.mean(widened, axis=-1, keepdims=True)
    shifted = widened - center
    variance = jnp.mean(shifted * shifted, axis=-1, keepdims=True)
    return shifted * lax.rsqrt(variance + 1e-05) * norm_gain + norm_bias


def rotate_local(vectors, position, first_column):
    half_count = vectors.shape[-1] // 2
    doubled = (first_column + 2 * jnp.arange(half_count)) % HDIM
    exponent = doubled.astype(jnp.float32) / ROT
    frequency = jnp.where(doubled < ROT, jnp.exp(-exponent * math.log(10000.0)), 0.0)
    angles = position[..., None] * frequency
    cosine = jnp.cos(angles)
    sine_part = jnp.sin(angles)
    halves = vectors.reshape(vectors.shape[:-1] + (half_count, 2))
    even_part = halves[..., 0]
    odd_part = halves[..., 1]
    turned = jnp.stack(
        [even_part * cosine - odd_part * sine_part, odd_part * cosine + even_part * sine_part],
        axis=-1,
    )
    return turned.reshape(vectors.shape)


def on_device(
    inputs,
    norm_gain,
    norm_bias,
    qkv_weight,
    out_weight,
    in_weight,
    in_bias,
    down_weight,
    down_bias,
    page_pool,
    old_cache,
    page_table,
    prompt_length,
    parents,
):
    batch_index = lax.axis_index("batch")
    tensor_index = lax.axis_index("tensor")
    groups = lax.axis_size("batch")
    steps = inputs.shape[0]
    model_width = inputs.shape[3]
    columns = qkv_weight.shape[2]
    requests = page_table.shape[0]
    history = old_cache.shape[3]
    page_count = page_table.shape[1]
    page_size = page_pool.shape[2]
    pool_dev = page_pool.shape[0]
    prompt_span = page_count * page_size
    local_reqs = requests // groups
    scale_factor = HDIM ** (-0.5)
    first_column = tensor_index * columns

    table_local = lax.dynamic_index_in_dim(
        page_table.reshape(local_reqs, groups, page_count), batch_index, 1, False
    ) - batch_index * pool_dev
    table_local = jnp.clip(table_local, 0, pool_dev - 1)
    length_local = lax.dynamic_index_in_dim(
        prompt_length.reshape(local_reqs, groups), batch_index, 1, False
    )
    pages = page_pool[table_local]
    prompt_keys = pages[:, :, 0].reshape(local_reqs, prompt_span, columns)
    prompt_values = pages[:, :, 1].reshape(local_reqs, prompt_span, columns)
    old_keys = old_cache[0, :, 0]
    other_old, other_prompt = partner((old_keys, prompt_keys), "tensor", 0)
    old_keys_full = jnp.concatenate([old_keys, other_old], axis=-1)
    prompt_keys_full = jnp.concatenate([prompt_keys, other_prompt], axis=-1)

    normed = normalize(inputs[:, 0], norm_gain, norm_bias).astype(jnp.bfloat16)
    rows = jnp.concatenate(
        [
            tree_all_gather(piece, "tensor", order, 1)
            for piece, order in zip(split_last(normed[:, 0], len(GATHER_ORDERS)), GATHER_ORDERS)
        ],
        axis=-1,
    )
    flat = rows.reshape(steps * requests, model_width)
    qkv_flat = qkv_weight.reshape(model_width, 3 * columns)
    projected = jnp.dot(flat, qkv_flat, preferred_element_type=jnp.float32).reshape(
        steps, requests, 3 * columns
    )
    ffn = jnp.dot(flat, in_weight, preferred_element_type=jnp.float32).reshape(
        steps, requests, -1
    )
    hidden = jax.nn.gelu(ffn + in_bias, approximate=True).astype(jnp.bfloat16)
    ffn_update = lax.optimization_barrier(
        jnp.einsum("srf,fd->rsd", hidden, down_weight, preferred_element_type=jnp.float32)
    )

    position = (
        prompt_length[None, :] + history + jnp.arange(steps, dtype=jnp.int32)[:, None]
    ).astype(jnp.float32)
    queries = rotate_local(projected[..., :columns], position, first_column).astype(jnp.bfloat16)
    fresh_keys = rotate_local(
        projected[..., columns : 2 * columns], position, first_column
    ).astype(jnp.bfloat16)
    fresh_values = projected[..., 2 * columns :].astype(jnp.bfloat16)

    other_q, other_k = partner((queries, fresh_keys), "tensor", 0)
    query_full = jnp.concatenate([queries, other_q], axis=-1)
    fresh_keys_full = jnp.concatenate([fresh_keys, other_k], axis=-1)

    query_all = lax.all_gather(query_full[:, None], "batch", axis=1, tiled=True)

    beam_ids = jnp.broadcast_to(jnp.arange(BEAMS, dtype=jnp.int32)[:, None], (BEAMS, requests))
    choices = jnp.arange(BEAMS, dtype=jnp.int32)[None, :, None]
    new_ok_steps = []
    old_ok_steps = []
    lineage = None
    for step_index in range(steps):
        pick = parents[step_index][:, None, :] == choices
        if lineage is None:
            root = parents[0]
            earlier = None
        else:
            stacked = jnp.concatenate([earlier, root[None]], axis=0)
            moved = jnp.sum(jnp.where(pick[None], stacked[:, None], 0), axis=2)
            earlier, root = moved[:-1], moved[-1]
        own = beam_ids[None]
        earlier = own if earlier is None else jnp.concatenate([earlier, own], axis=0)
        lineage = earlier
        hit = earlier == batch_index
        if step_index + 1 < steps:
            hit = jnp.concatenate(
                [hit, jnp.zeros((steps - 1 - step_index, BEAMS, requests), bool)], axis=0
            )
        new_ok_steps.append(jnp.moveaxis(hit, 0, -1))
        old_ok_steps.append(root == batch_index)
    new_ok = jnp.stack(new_ok_steps, axis=0)
    old_ok = jnp.stack(old_ok_steps, axis=0)

    old_values = old_cache[0, :, 1]
    old_scores = jnp.einsum(
        "sbrc,rhc->sbrh", query_all, old_keys_full, preferred_element_type=jnp.float32
    ) * scale_factor
    new_scores = jnp.einsum(
        "sbrc,trc->sbrt", query_all, fresh_keys_full, preferred_element_type=jnp.float32
    ) * scale_factor

    query_local = lax.dynamic_index_in_dim(
        query_all.reshape(steps, BEAMS, local_reqs, groups, 2 * columns), batch_index, 3, False
    )
    prompt_scores = jnp.einsum(
        "sbrc,rtc->sbrt", query_local, prompt_keys_full, preferred_element_type=jnp.float32
    ) * scale_factor

    old_mask = old_ok[..., None]
    old_masked = jnp.where(old_mask, old_scores, NEG_FILL)
    new_masked = jnp.where(new_ok, new_scores, NEG_FILL)
    chain_peak = jnp.maximum(jnp.max(old_masked, axis=-1), jnp.max(new_masked, axis=-1))
    old_w = jnp.where(old_mask, jnp.exp(old_masked - chain_peak[..., None]), 0.0)
    new_w = jnp.where(new_ok, jnp.exp(new_masked - chain_peak[..., None]), 0.0)
    chain_total = jnp.sum(old_w, axis=-1) + jnp.sum(new_w, axis=-1)
    chain_mix = jnp.einsum(
        "sbrh,rhc->sbrc", old_w.astype(jnp.bfloat16), old_values, preferred_element_type=jnp.float32
    ) + jnp.einsum(
        "sbrt,trc->sbrc",
        new_w.astype(jnp.bfloat16),
        fresh_values,
        preferred_element_type=jnp.float32,
    )

    prompt_mask = (jnp.arange(prompt_span)[None, :] < length_local[:, None])[None, None]
    prompt_masked = jnp.where(prompt_mask, prompt_scores, NEG_FILL)
    prompt_peak = jnp.max(prompt_masked, axis=-1)
    prompt_w = jnp.where(prompt_mask, jnp.exp(prompt_masked - prompt_peak[..., None]), 0.0)
    prompt_total = jnp.sum(prompt_w, axis=-1)
    prompt_mix = jnp.einsum(
        "sbrt,rtc->sbrc",
        prompt_w.astype(jnp.bfloat16),
        prompt_values,
        preferred_element_type=jnp.float32,
    )

    slot_hit = (jnp.arange(groups) == batch_index)[None, None, None, :]
    def spread(values, fill):
        placed = jnp.where(slot_hit, values[..., None], fill)
        return placed.reshape(values.shape[:2] + (requests,))

    def spread_mix(values):
        placed = jnp.where(slot_hit[..., None], values[:, :, :, None, :], 0.0)
        return placed.reshape(values.shape[:2] + (requests, columns))

    p_peak = spread(prompt_peak, NEG_FILL)
    p_total = spread(prompt_total, 0.0)
    p_mix = spread_mix(prompt_mix)
    peak = jnp.maximum(chain_peak, p_peak)
    f_chain = jnp.exp(chain_peak - peak)
    f_prompt = jnp.exp(p_peak - peak)
    total = chain_total * f_chain + p_total * f_prompt
    mix = chain_mix * f_chain[..., None] + p_mix * f_prompt[..., None]

    packed = jnp.concatenate([mix, peak[..., None], total[..., None]], axis=-1)
    received = lax.all_to_all(packed, "batch", 1, 1, tiled=True)
    r_mix = received[..., :columns]
    r_peak = received[..., columns]
    r_total = received[..., columns + 1]
    g_peak = jnp.max(r_peak, axis=1, keepdims=True)
    factor = jnp.exp(r_peak - g_peak)
    all_total = jnp.sum(r_total * factor, axis=1)
    all_mix = jnp.sum(r_mix * factor[..., None], axis=1)
    attention = (all_mix / all_total[..., None]).astype(jnp.bfloat16)

    update = (
        jnp.einsum("src,cd->rsd", attention, out_weight, preferred_element_type=jnp.float32)
        + ffn_update
    )
    summed = jnp.concatenate(
        [
            tree_reduce_scatter(piece, "tensor", order)
            for piece, order in zip(split_last(update, len(SCATTER_ORDERS)), SCATTER_ORDERS)
        ],
        axis=-1,
    )
    result = inputs[:, 0].astype(jnp.float32) + summed[:, None] + down_bias
    return result[:, None]


def solution(mesh):
    in_specs = (
        P(None, "batch", "tensor", None),
        P(),
        P(),
        P(None, None, "tensor"),
        P("tensor", None),
        P(None, "tensor"),
        P("tensor"),
        P("tensor", None),
        P(),
        P("batch", None, None, "tensor"),
        P("batch", None, None, None, "tensor"),
        P(),
        P(),
        P(),
    )
    out_specs = P(None, "batch", "tensor", None)
    return jax.shard_map(
        on_device, mesh=mesh, in_specs=in_specs, out_specs=out_specs, check_vma=False
    )
```

```python
import math

import jax
import jax.numpy as jnp
from jax import lax
from jax.sharding import PartitionSpec as P

HDIM = 256
ROT = 64
BEAMS = 8

NEG_FILL = -1e30
LINK_TYPE = jnp.bfloat16
SCATTER_ORDERS = ((0, 3, 1, 4, 2), (3, 0, 4, 1, 2))
GATHER_ORDERS = ((2, 4, 1, 3, 0), (2, 1, 4, 0, 3))


def partner(value, axis, bit):
    return lax.ppermute(value, axis, [(i, i ^ 1 << bit) for i in range(lax.axis_size(axis))])


def tree_reduce_scatter(x, axis, order):
    n = x.shape[0]
    nbits = n.bit_length() - 1
    me = lax.axis_index(axis)
    x = x.reshape((2,) * nbits + x.shape[1:])
    remaining = list(range(nbits - 1, -1, -1))
    for k in order:
        a = remaining.index(k)
        bit = (me >> k) & 1
        keep = lax.dynamic_index_in_dim(x, bit, a, keepdims=False)
        send = lax.dynamic_index_in_dim(x, 1 - bit, a, keepdims=False).astype(LINK_TYPE)
        x = keep + partner(send, axis, k).astype(keep.dtype)
        remaining.pop(a)
    return x


def tree_all_gather(x, axis, order, out_axis):
    n = lax.axis_size(axis)
    nbits = n.bit_length() - 1
    me = lax.axis_index(axis)
    have = []
    for k in order:
        bit = (me >> k) & 1
        got = partner(x, axis, k)
        low = jnp.where(bit == 0, x, got)
        high = jnp.where(bit == 0, got, x)
        x = jnp.stack([low, high], axis=0)
        have.insert(0, k)
    rest = list(range(nbits, x.ndim))
    lead = [have.index(b) for b in range(nbits - 1, -1, -1)]
    perm = rest[:out_axis] + lead + rest[out_axis:]
    x = jnp.transpose(x, perm)
    return x.reshape(x.shape[:out_axis] + (n,) + x.shape[out_axis + nbits :])


def split_last(x, count):
    width = x.shape[-1] // count
    return [x[..., i * width : (i + 1) * width] for i in range(count)]


def normalize(row_block, norm_gain, norm_bias):
    widened = row_block.astype(jnp.float32)
    center = jnp.mean(widened, axis=-1, keepdims=True)
    shifted = widened - center
    variance = jnp.mean(shifted * shifted, axis=-1, keepdims=True)
    return shifted * lax.rsqrt(variance + 1e-05) * norm_gain + norm_bias


def rotate_local(vectors, position, first_column):
    half_count = vectors.shape[-1] // 2
    doubled = (first_column + 2 * jnp.arange(half_count)) % HDIM
    exponent = doubled.astype(jnp.float32) / ROT
    frequency = jnp.where(doubled < ROT, jnp.exp(-exponent * math.log(10000.0)), 0.0)
    angles = position[..., None] * frequency
    cosine = jnp.cos(angles)
    sine_part = jnp.sin(angles)
    halves = vectors.reshape(vectors.shape[:-1] + (half_count, 2))
    even_part = halves[..., 0]
    odd_part = halves[..., 1]
    turned = jnp.stack(
        [even_part * cosine - odd_part * sine_part, odd_part * cosine + even_part * sine_part],
        axis=-1,
    )
    return turned.reshape(vectors.shape)


def on_device(
    inputs,
    norm_gain,
    norm_bias,
    qkv_weight,
    out_weight,
    in_weight,
    in_bias,
    down_weight,
    down_bias,
    page_pool,
    old_cache,
    page_table,
    prompt_length,
    parents,
):
    batch_index = lax.axis_index("batch")
    tensor_index = lax.axis_index("tensor")
    groups = lax.axis_size("batch")
    steps = inputs.shape[0]
    model_width = inputs.shape[3]
    columns = qkv_weight.shape[2]
    requests = page_table.shape[0]
    history = old_cache.shape[3]
    page_count = page_table.shape[1]
    page_size = page_pool.shape[2]
    pool_dev = page_pool.shape[0]
    prompt_span = page_count * page_size
    local_reqs = requests // groups
    scale_factor = HDIM ** (-0.5)
    first_column = tensor_index * columns

    table_local = lax.dynamic_index_in_dim(
        page_table.reshape(local_reqs, groups, page_count), batch_index, 1, False
    ) - batch_index * pool_dev
    table_local = jnp.clip(table_local, 0, pool_dev - 1)
    length_local = lax.dynamic_index_in_dim(
        prompt_length.reshape(local_reqs, groups), batch_index, 1, False
    )
    pages = page_pool[table_local]
    prompt_keys = pages[:, :, 0].reshape(local_reqs, prompt_span, columns)
    prompt_values = pages[:, :, 1].reshape(local_reqs, prompt_span, columns)
    old_keys = old_cache[0, :, 0]
    other_old, other_prompt = partner((old_keys, prompt_keys), "tensor", 0)
    old_keys_full = jnp.concatenate([old_keys, other_old], axis=-1)
    prompt_keys_full = jnp.concatenate([prompt_keys, other_prompt], axis=-1)

    normed = normalize(inputs[:, 0], norm_gain, norm_bias).astype(jnp.bfloat16)
    row_parts = [
        tree_all_gather(piece, "tensor", order, 1).reshape(steps * requests, -1)
        for piece, order in zip(split_last(normed[:, 0], len(GATHER_ORDERS)), GATHER_ORDERS)
    ]
    part_width = model_width // len(row_parts)
    qkv_flat = qkv_weight.reshape(model_width, 3 * columns)
    projected = sum(
        jnp.dot(
            part, qkv_flat[i * part_width : (i + 1) * part_width], preferred_element_type=jnp.float32
        )
        for i, part in enumerate(row_parts)
    ).reshape(steps, requests, 3 * columns)
    ffn = sum(
        jnp.dot(
            part, in_weight[i * part_width : (i + 1) * part_width], preferred_element_type=jnp.float32
        )
        for i, part in enumerate(row_parts)
    ).reshape(steps, requests, -1)
    hidden = jax.nn.gelu(ffn + in_bias, approximate=True).astype(jnp.bfloat16)
    ffn_update = lax.optimization_barrier(
        jnp.einsum("srf,fd->rsd", hidden, down_weight, preferred_element_type=jnp.float32)
    )

    position = (
        prompt_length[None, :] + history + jnp.arange(steps, dtype=jnp.int32)[:, None]
    ).astype(jnp.float32)
    queries = rotate_local(projected[..., :columns], position, first_column).astype(jnp.bfloat16)
    fresh_keys = rotate_local(
        projected[..., columns : 2 * columns], position, first_column
    ).astype(jnp.bfloat16)
    fresh_values = projected[..., 2 * columns :].astype(jnp.bfloat16)

    other_q, other_k = partner((queries, fresh_keys), "tensor", 0)
    query_full = jnp.concatenate([queries, other_q], axis=-1)
    fresh_keys_full = jnp.concatenate([fresh_keys, other_k], axis=-1)

    query_all = lax.all_gather(query_full[:, None], "batch", axis=1, tiled=True)

    beam_ids = jnp.broadcast_to(jnp.arange(BEAMS, dtype=jnp.int32)[:, None], (BEAMS, requests))
    choices = jnp.arange(BEAMS, dtype=jnp.int32)[None, :, None]
    new_ok_steps = []
    old_ok_steps = []
    lineage = None
    for step_index in range(steps):
        pick = parents[step_index][:, None, :] == choices
        if lineage is None:
            root = parents[0]
            earlier = None
        else:
            stacked = jnp.concatenate([earlier, root[None]], axis=0)
            moved = jnp.sum(jnp.where(pick[None], stacked[:, None], 0), axis=2)
            earlier, root = moved[:-1], moved[-1]
        own = beam_ids[None]
        earlier = own if earlier is None else jnp.concatenate([earlier, own], axis=0)
        lineage = earlier
        hit = earlier == batch_index
        if step_index + 1 < steps:
            hit = jnp.concatenate(
                [hit, jnp.zeros((steps - 1 - step_index, BEAMS, requests), bool)], axis=0
            )
        new_ok_steps.append(jnp.moveaxis(hit, 0, -1))
        old_ok_steps.append(root == batch_index)
    new_ok = jnp.stack(new_ok_steps, axis=0)
    old_ok = jnp.stack(old_ok_steps, axis=0)

    old_values = old_cache[0, :, 1]
    old_scores = jnp.einsum(
        "sbrc,rhc->sbrh", query_all, old_keys_full, preferred_element_type=jnp.float32
    ) * scale_factor
    new_scores = jnp.einsum(
        "sbrc,trc->sbrt", query_all, fresh_keys_full, preferred_element_type=jnp.float32
    ) * scale_factor

    query_local = lax.dynamic_index_in_dim(
        query_all.reshape(steps, BEAMS, local_reqs, groups, 2 * columns), batch_index, 3, False
    )
    prompt_scores = jnp.einsum(
        "sbrc,rtc->sbrt", query_local, prompt_keys_full, preferred_element_type=jnp.float32
    ) * scale_factor

    old_mask = old_ok[..., None]
    old_masked = jnp.where(old_mask, old_scores, NEG_FILL)
    new_masked = jnp.where(new_ok, new_scores, NEG_FILL)
    chain_peak = jnp.maximum(jnp.max(old_masked, axis=-1), jnp.max(new_masked, axis=-1))
    old_w = jnp.where(old_mask, jnp.exp(old_masked - chain_peak[..., None]), 0.0)
    new_w = jnp.where(new_ok, jnp.exp(new_masked - chain_peak[..., None]), 0.0)
    chain_total = jnp.sum(old_w, axis=-1) + jnp.sum(new_w, axis=-1)
    chain_mix = jnp.einsum(
        "sbrh,rhc->sbrc", old_w.astype(jnp.bfloat16), old_values, preferred_element_type=jnp.float32
    ) + jnp.einsum(
        "sbrt,trc->sbrc",
        new_w.astype(jnp.bfloat16),
        fresh_values,
        preferred_element_type=jnp.float32,
    )

    prompt_mask = (jnp.arange(prompt_span)[None, :] < length_local[:, None])[None, None]
    prompt_masked = jnp.where(prompt_mask, prompt_scores, NEG_FILL)
    prompt_peak = jnp.max(prompt_masked, axis=-1)
    prompt_w = jnp.where(prompt_mask, jnp.exp(prompt_masked - prompt_peak[..., None]), 0.0)
    prompt_total = jnp.sum(prompt_w, axis=-1)
    prompt_mix = jnp.einsum(
        "sbrt,rtc->sbrc",
        prompt_w.astype(jnp.bfloat16),
        prompt_values,
        preferred_element_type=jnp.float32,
    )

    slot_hit = (jnp.arange(groups) == batch_index)[None, None, None, :]
    def spread(values, fill):
        placed = jnp.where(slot_hit, values[..., None], fill)
        return placed.reshape(values.shape[:2] + (requests,))

    def spread_mix(values):
        placed = jnp.where(slot_hit[..., None], values[:, :, :, None, :], 0.0)
        return placed.reshape(values.shape[:2] + (requests, columns))

    p_peak = spread(prompt_peak, NEG_FILL)
    p_total = spread(prompt_total, 0.0)
    p_mix = spread_mix(prompt_mix)
    peak = jnp.maximum(chain_peak, p_peak)
    f_chain = jnp.exp(chain_peak - peak)
    f_prompt = jnp.exp(p_peak - peak)
    total = chain_total * f_chain + p_total * f_prompt
    mix = chain_mix * f_chain[..., None] + p_mix * f_prompt[..., None]

    packed = jnp.concatenate([mix, peak[..., None], total[..., None]], axis=-1)
    received = lax.all_to_all(packed, "batch", 1, 1, tiled=True)
    r_mix = received[..., :columns]
    r_peak = received[..., columns]
    r_total = received[..., columns + 1]
    g_peak = jnp.max(r_peak, axis=1, keepdims=True)
    factor = jnp.exp(r_peak - g_peak)
    all_total = jnp.sum(r_total * factor, axis=1)
    all_mix = jnp.sum(r_mix * factor[..., None], axis=1)
    attention = (all_mix / all_total[..., None]).astype(jnp.bfloat16)

    update = (
        jnp.einsum("src,cd->rsd", attention, out_weight, preferred_element_type=jnp.float32)
        + ffn_update
    )
    summed = jnp.concatenate(
        [
            tree_reduce_scatter(piece, "tensor", order)
            for piece, order in zip(split_last(update, len(SCATTER_ORDERS)), SCATTER_ORDERS)
        ],
        axis=-1,
    )
    result = inputs[:, 0].astype(jnp.float32) + summed[:, None] + down_bias
    return result[:, None]


def solution(mesh):
    in_specs = (
        P(None, "batch", "tensor", None),
        P(),
        P(),
        P(None, None, "tensor"),
        P("tensor", None),
        P(None, "tensor"),
        P("tensor"),
        P("tensor", None),
        P(),
        P("batch", None, None, "tensor"),
        P("batch", None, None, None, "tensor"),
        P(),
        P(),
        P(),
    )
    out_specs = P(None, "batch", "tensor", None)
    return jax.shard_map(
        on_device, mesh=mesh, in_specs=in_specs, out_specs=out_specs, check_vma=False
    )
```

```python
import math

import jax
import jax.numpy as jnp
from jax import lax
from jax.sharding import PartitionSpec as P

HDIM = 256
ROT = 64
BEAMS = 8

NEG_FILL = -1e30
LINK_TYPE = jnp.bfloat16
SCATTER_ORDERS = ((0, 3, 1, 4, 2), (3, 0, 4, 1, 2))
GATHER_ORDERS = ((2, 4, 1, 3, 0), (2, 1, 4, 0, 3))


def partner(value, axis, bit):
    return lax.ppermute(value, axis, [(i, i ^ 1 << bit) for i in range(lax.axis_size(axis))])


def tree_reduce_scatter(x, axis, order):
    n = x.shape[0]
    nbits = n.bit_length() - 1
    me = lax.axis_index(axis)
    x = x.reshape((2,) * nbits + x.shape[1:])
    remaining = list(range(nbits - 1, -1, -1))
    for k in order:
        a = remaining.index(k)
        bit = (me >> k) & 1
        keep = lax.dynamic_index_in_dim(x, bit, a, keepdims=False)
        send = lax.dynamic_index_in_dim(x, 1 - bit, a, keepdims=False).astype(LINK_TYPE)
        x = keep + partner(send, axis, k).astype(keep.dtype)
        remaining.pop(a)
    return x


def tree_all_gather(x, axis, order, out_axis, taps=None):
    n = lax.axis_size(axis)
    nbits = n.bit_length() - 1
    me = lax.axis_index(axis)
    have = []
    for k in order:
        bit = (me >> k) & 1
        got = partner(x, axis, k)
        low = jnp.where(bit == 0, x, got)
        high = jnp.where(bit == 0, got, x)
        x = jnp.stack([low, high], axis=0)
        have.insert(0, k)
        if taps is not None:
            taps.append(x)
    rest = list(range(nbits, x.ndim))
    lead = [have.index(b) for b in range(nbits - 1, -1, -1)]
    perm = rest[:out_axis] + lead + rest[out_axis:]
    x = jnp.transpose(x, perm)
    return x.reshape(x.shape[:out_axis] + (n,) + x.shape[out_axis + nbits :])


def split_last(x, count):
    width = x.shape[-1] // count
    return [x[..., i * width : (i + 1) * width] for i in range(count)]


def normalize(row_block, norm_gain, norm_bias):
    widened = row_block.astype(jnp.float32)
    center = jnp.mean(widened, axis=-1, keepdims=True)
    shifted = widened - center
    variance = jnp.mean(shifted * shifted, axis=-1, keepdims=True)
    return shifted * lax.rsqrt(variance + 1e-05) * norm_gain + norm_bias


def rotate_local(vectors, position, first_column):
    half_count = vectors.shape[-1] // 2
    doubled = (first_column + 2 * jnp.arange(half_count)) % HDIM
    exponent = doubled.astype(jnp.float32) / ROT
    frequency = jnp.where(doubled < ROT, jnp.exp(-exponent * math.log(10000.0)), 0.0)
    angles = position[..., None] * frequency
    cosine = jnp.cos(angles)
    sine_part = jnp.sin(angles)
    halves = vectors.reshape(vectors.shape[:-1] + (half_count, 2))
    even_part = halves[..., 0]
    odd_part = halves[..., 1]
    turned = jnp.stack(
        [even_part * cosine - odd_part * sine_part, odd_part * cosine + even_part * sine_part],
        axis=-1,
    )
    return turned.reshape(vectors.shape)


def on_device(
    inputs,
    norm_gain,
    norm_bias,
    qkv_weight,
    out_weight,
    in_weight,
    in_bias,
    down_weight,
    down_bias,
    page_pool,
    old_cache,
    page_table,
    prompt_length,
    parents,
):
    batch_index = lax.axis_index("batch")
    tensor_index = lax.axis_index("tensor")
    groups = lax.axis_size("batch")
    steps = inputs.shape[0]
    model_width = inputs.shape[3]
    columns = qkv_weight.shape[2]
    requests = page_table.shape[0]
    history = old_cache.shape[3]
    page_count = page_table.shape[1]
    page_size = page_pool.shape[2]
    pool_dev = page_pool.shape[0]
    prompt_span = page_count * page_size
    local_reqs = requests // groups
    scale_factor = HDIM ** (-0.5)
    first_column = tensor_index * columns

    table_local = lax.dynamic_index_in_dim(
        page_table.reshape(local_reqs, groups, page_count), batch_index, 1, False
    ) - batch_index * pool_dev
    table_local = jnp.clip(table_local, 0, pool_dev - 1)
    length_local = lax.dynamic_index_in_dim(
        prompt_length.reshape(local_reqs, groups), batch_index, 1, False
    )
    pages = page_pool[table_local]
    prompt_keys = pages[:, :, 0].reshape(local_reqs, prompt_span, columns)
    prompt_values = pages[:, :, 1].reshape(local_reqs, prompt_span, columns)
    old_keys = old_cache[0, :, 0]
    other_old = partner(old_keys, "tensor", 0)
    old_keys_full = jnp.concatenate([old_keys, other_old], axis=-1)

    normed = normalize(inputs[:, 0], norm_gain, norm_bias).astype(jnp.bfloat16)
    taps = []
    rows = jnp.concatenate(
        [
            tree_all_gather(piece, "tensor", order, 1, taps if i == 0 else None)
            for i, (piece, order) in enumerate(
                zip(split_last(normed[:, 0], len(GATHER_ORDERS)), GATHER_ORDERS)
            )
        ],
        axis=-1,
    )
    prompt_keys_late, _ = lax.optimization_barrier((prompt_keys, taps[1]))
    other_prompt = partner(prompt_keys_late, "tensor", 0)
    prompt_keys_full = jnp.concatenate([prompt_keys, other_prompt], axis=-1)
    flat = rows.reshape(steps * requests, model_width)
    qkv_flat = qkv_weight.reshape(model_width, 3 * columns)
    projected = jnp.dot(flat, qkv_flat, preferred_element_type=jnp.float32).reshape(
        steps, requests, 3 * columns
    )
    ffn = jnp.dot(flat, in_weight, preferred_element_type=jnp.float32).reshape(
        steps, requests, -1
    )
    hidden = jax.nn.gelu(ffn + in_bias, approximate=True).astype(jnp.bfloat16)
    ffn_update = lax.optimization_barrier(
        jnp.einsum("srf,fd->rsd", hidden, down_weight, preferred_element_type=jnp.float32)
    )

    position = (
        prompt_length[None, :] + history + jnp.arange(steps, dtype=jnp.int32)[:, None]
    ).astype(jnp.float32)
    queries = rotate_local(projected[..., :columns], position, first_column).astype(jnp.bfloat16)
    fresh_keys = rotate_local(
        projected[..., columns : 2 * columns], position, first_column
    ).astype(jnp.bfloat16)
    fresh_values = projected[..., 2 * columns :].astype(jnp.bfloat16)

    other_q, other_k = partner((queries, fresh_keys), "tensor", 0)
    query_full = jnp.concatenate([queries, other_q], axis=-1)
    fresh_keys_full = jnp.concatenate([fresh_keys, other_k], axis=-1)

    query_all = lax.all_gather(query_full[:, None], "batch", axis=1, tiled=True)

    beam_ids = jnp.broadcast_to(jnp.arange(BEAMS, dtype=jnp.int32)[:, None], (BEAMS, requests))
    choices = jnp.arange(BEAMS, dtype=jnp.int32)[None, :, None]
    new_ok_steps = []
    old_ok_steps = []
    lineage = None
    for step_index in range(steps):
        pick = parents[step_index][:, None, :] == choices
        if lineage is None:
            root = parents[0]
            earlier = None
        else:
            stacked = jnp.concatenate([earlier, root[None]], axis=0)
            moved = jnp.sum(jnp.where(pick[None], stacked[:, None], 0), axis=2)
            earlier, root = moved[:-1], moved[-1]
        own = beam_ids[None]
        earlier = own if earlier is None else jnp.concatenate([earlier, own], axis=0)
        lineage = earlier
        hit = earlier == batch_index
        if step_index + 1 < steps:
            hit = jnp.concatenate(
                [hit, jnp.zeros((steps - 1 - step_index, BEAMS, requests), bool)], axis=0
            )
        new_ok_steps.append(jnp.moveaxis(hit, 0, -1))
        old_ok_steps.append(root == batch_index)
    new_ok = jnp.stack(new_ok_steps, axis=0)
    old_ok = jnp.stack(old_ok_steps, axis=0)

    old_values = old_cache[0, :, 1]
    old_scores = jnp.einsum(
        "sbrc,rhc->sbrh", query_all, old_keys_full, preferred_element_type=jnp.float32
    ) * scale_factor
    new_scores = jnp.einsum(
        "sbrc,trc->sbrt", query_all, fresh_keys_full, preferred_element_type=jnp.float32
    ) * scale_factor

    query_local = lax.dynamic_index_in_dim(
        query_all.reshape(steps, BEAMS, local_reqs, groups, 2 * columns), batch_index, 3, False
    )
    prompt_scores = jnp.einsum(
        "sbrc,rtc->sbrt", query_local, prompt_keys_full, preferred_element_type=jnp.float32
    ) * scale_factor

    old_mask = old_ok[..., None]
    old_masked = jnp.where(old_mask, old_scores, NEG_FILL)
    new_masked = jnp.where(new_ok, new_scores, NEG_FILL)
    chain_peak = jnp.maximum(jnp.max(old_masked, axis=-1), jnp.max(new_masked, axis=-1))
    old_w = jnp.where(old_mask, jnp.exp(old_masked - chain_peak[..., None]), 0.0)
    new_w = jnp.where(new_ok, jnp.exp(new_masked - chain_peak[..., None]), 0.0)
    chain_total = jnp.sum(old_w, axis=-1) + jnp.sum(new_w, axis=-1)
    chain_mix = jnp.einsum(
        "sbrh,rhc->sbrc", old_w.astype(jnp.bfloat16), old_values, preferred_element_type=jnp.float32
    ) + jnp.einsum(
        "sbrt,trc->sbrc",
        new_w.astype(jnp.bfloat16),
        fresh_values,
        preferred_element_type=jnp.float32,
    )

    prompt_mask = (jnp.arange(prompt_span)[None, :] < length_local[:, None])[None, None]
    prompt_masked = jnp.where(prompt_mask, prompt_scores, NEG_FILL)
    prompt_peak = jnp.max(prompt_masked, axis=-1)
    prompt_w = jnp.where(prompt_mask, jnp.exp(prompt_masked - prompt_peak[..., None]), 0.0)
    prompt_total = jnp.sum(prompt_w, axis=-1)
    prompt_mix = jnp.einsum(
        "sbrt,rtc->sbrc",
        prompt_w.astype(jnp.bfloat16),
        prompt_values,
        preferred_element_type=jnp.float32,
    )

    slot_hit = (jnp.arange(groups) == batch_index)[None, None, None, :]
    def spread(values, fill):
        placed = jnp.where(slot_hit, values[..., None], fill)
        return placed.reshape(values.shape[:2] + (requests,))

    def spread_mix(values):
        placed = jnp.where(slot_hit[..., None], values[:, :, :, None, :], 0.0)
        return placed.reshape(values.shape[:2] + (requests, columns))

    p_peak = spread(prompt_peak, NEG_FILL)
    p_total = spread(prompt_total, 0.0)
    p_mix = spread_mix(prompt_mix)
    peak = jnp.maximum(chain_peak, p_peak)
    f_chain = jnp.exp(chain_peak - peak)
    f_prompt = jnp.exp(p_peak - peak)
    total = chain_total * f_chain + p_total * f_prompt
    mix = chain_mix * f_chain[..., None] + p_mix * f_prompt[..., None]

    packed = jnp.concatenate([mix, peak[..., None], total[..., None]], axis=-1)
    received = lax.all_to_all(packed, "batch", 1, 1, tiled=True)
    r_mix = received[..., :columns]
    r_peak = received[..., columns]
    r_total = received[..., columns + 1]
    g_peak = jnp.max(r_peak, axis=1, keepdims=True)
    factor = jnp.exp(r_peak - g_peak)
    all_total = jnp.sum(r_total * factor, axis=1)
    all_mix = jnp.sum(r_mix * factor[..., None], axis=1)
    attention = (all_mix / all_total[..., None]).astype(jnp.bfloat16)

    update = (
        jnp.einsum("src,cd->rsd", attention, out_weight, preferred_element_type=jnp.float32)
        + ffn_update
    )
    summed = jnp.concatenate(
        [
            tree_reduce_scatter(piece, "tensor", order)
            for piece, order in zip(split_last(update, len(SCATTER_ORDERS)), SCATTER_ORDERS)
        ],
        axis=-1,
    )
    result = inputs[:, 0].astype(jnp.float32) + summed[:, None] + down_bias
    return result[:, None]


def solution(mesh):
    in_specs = (
        P(None, "batch", "tensor", None),
        P(),
        P(),
        P(None, None, "tensor"),
        P("tensor", None),
        P(None, "tensor"),
        P("tensor"),
        P("tensor", None),
        P(),
        P("batch", None, None, "tensor"),
        P("batch", None, None, None, "tensor"),
        P(),
        P(),
        P(),
    )
    out_specs = P(None, "batch", "tensor", None)
    return jax.shard_map(
        on_device, mesh=mesh, in_specs=in_specs, out_specs=out_specs, check_vma=False
    )
```

```python
import math

import jax
import jax.numpy as jnp
from jax import lax
from jax.sharding import PartitionSpec as P

HDIM = 256
ROT = 64
BEAMS = 8

NEG_FILL = -1e30
LINK_TYPE = jnp.bfloat16
SCATTER_ORDERS = ((0, 3, 1, 4, 2), (3, 0, 4, 2, 1))
GATHER_ORDERS = ((2, 4, 1, 3, 0), (2, 1, 4, 0, 3))


def partner(value, axis, bit):
    return lax.ppermute(value, axis, [(i, i ^ 1 << bit) for i in range(lax.axis_size(axis))])


def tree_reduce_scatter(x, axis, order):
    n = x.shape[0]
    nbits = n.bit_length() - 1
    me = lax.axis_index(axis)
    x = x.reshape((2,) * nbits + x.shape[1:])
    remaining = list(range(nbits - 1, -1, -1))
    for k in order:
        a = remaining.index(k)
        bit = (me >> k) & 1
        keep = lax.dynamic_index_in_dim(x, bit, a, keepdims=False)
        send = lax.dynamic_index_in_dim(x, 1 - bit, a, keepdims=False).astype(LINK_TYPE)
        x = keep + partner(send, axis, k).astype(keep.dtype)
        remaining.pop(a)
    return x


def tree_all_gather(x, axis, order, out_axis):
    n = lax.axis_size(axis)
    nbits = n.bit_length() - 1
    me = lax.axis_index(axis)
    have = []
    for k in order:
        bit = (me >> k) & 1
        got = partner(x, axis, k)
        low = jnp.where(bit == 0, x, got)
        high = jnp.where(bit == 0, got, x)
        x = jnp.stack([low, high], axis=0)
        have.insert(0, k)
    rest = list(range(nbits, x.ndim))
    lead = [have.index(b) for b in range(nbits - 1, -1, -1)]
    perm = rest[:out_axis] + lead + rest[out_axis:]
    x = jnp.transpose(x, perm)
    return x.reshape(x.shape[:out_axis] + (n,) + x.shape[out_axis + nbits :])


def split_last(x, count):
    width = x.shape[-1] // count
    return [x[..., i * width : (i + 1) * width] for i in range(count)]


def normalize(row_block, norm_gain, norm_bias):
    widened = row_block.astype(jnp.float32)
    center = jnp.mean(widened, axis=-1, keepdims=True)
    shifted = widened - center
    variance = jnp.mean(shifted * shifted, axis=-1, keepdims=True)
    return shifted * lax.rsqrt(variance + 1e-05) * norm_gain + norm_bias


def rotate_local(vectors, position, first_column):
    half_count = vectors.shape[-1] // 2
    doubled = (first_column + 2 * jnp.arange(half_count)) % HDIM
    exponent = doubled.astype(jnp.float32) / ROT
    frequency = jnp.where(doubled < ROT, jnp.exp(-exponent * math.log(10000.0)), 0.0)
    angles = position[..., None] * frequency
    cosine = jnp.cos(angles)
    sine_part = jnp.sin(angles)
    halves = vectors.reshape(vectors.shape[:-1] + (half_count, 2))
    even_part = halves[..., 0]
    odd_part = halves[..., 1]
    turned = jnp.stack(
        [even_part * cosine - odd_part * sine_part, odd_part * cosine + even_part * sine_part],
        axis=-1,
    )
    return turned.reshape(vectors.shape)


def on_device(
    inputs,
    norm_gain,
    norm_bias,
    qkv_weight,
    out_weight,
    in_weight,
    in_bias,
    down_weight,
    down_bias,
    page_pool,
    old_cache,
    page_table,
    prompt_length,
    parents,
):
    batch_index = lax.axis_index("batch")
    tensor_index = lax.axis_index("tensor")
    groups = lax.axis_size("batch")
    steps = inputs.shape[0]
    model_width = inputs.shape[3]
    columns = qkv_weight.shape[2]
    requests = page_table.shape[0]
    history = old_cache.shape[3]
    page_count = page_table.shape[1]
    page_size = page_pool.shape[2]
    pool_dev = page_pool.shape[0]
    prompt_span = page_count * page_size
    local_reqs = requests // groups
    scale_factor = HDIM ** (-0.5)
    first_column = tensor_index * columns

    table_local = lax.dynamic_index_in_dim(
        page_table.reshape(local_reqs, groups, page_count), batch_index, 1, False
    ) - batch_index * pool_dev
    table_local = jnp.clip(table_local, 0, pool_dev - 1)
    length_local = lax.dynamic_index_in_dim(
        prompt_length.reshape(local_reqs, groups), batch_index, 1, False
    )
    pages = page_pool[table_local]
    prompt_keys = pages[:, :, 0].reshape(local_reqs, prompt_span, columns)
    prompt_values = pages[:, :, 1].reshape(local_reqs, prompt_span, columns)
    old_keys = old_cache[0, :, 0]
    other_old, other_prompt = partner((old_keys, prompt_keys), "tensor", 0)
    old_keys_full = jnp.concatenate([old_keys, other_old], axis=-1)
    prompt_keys_full = jnp.concatenate([prompt_keys, other_prompt], axis=-1)

    normed = normalize(inputs[:, 0], norm_gain, norm_bias).astype(jnp.bfloat16)
    rows = jnp.concatenate(
        [
            tree_all_gather(piece, "tensor", order, 1)
            for piece, order in zip(split_last(normed[:, 0], len(GATHER_ORDERS)), GATHER_ORDERS)
        ],
        axis=-1,
    )
    flat = rows.reshape(steps * requests, model_width)
    qkv_flat = qkv_weight.reshape(model_width, 3 * columns)
    projected = jnp.dot(flat, qkv_flat, preferred_element_type=jnp.float32).reshape(
        steps, requests, 3 * columns
    )
    ffn = jnp.dot(flat, in_weight, preferred_element_type=jnp.float32).reshape(
        steps, requests, -1
    )
    hidden = jax.nn.gelu(ffn + in_bias, approximate=True).astype(jnp.bfloat16)
    ffn_update = lax.optimization_barrier(
        jnp.einsum("srf,fd->rsd", hidden, down_weight, preferred_element_type=jnp.float32)
    )

    position = (
        prompt_length[None, :] + history + jnp.arange(steps, dtype=jnp.int32)[:, None]
    ).astype(jnp.float32)
    queries = rotate_local(projected[..., :columns], position, first_column).astype(jnp.bfloat16)
    fresh_keys = rotate_local(
        projected[..., columns : 2 * columns], position, first_column
    ).astype(jnp.bfloat16)
    fresh_values = projected[..., 2 * columns :].astype(jnp.bfloat16)

    other_q, other_k = partner((queries, fresh_keys), "tensor", 0)
    query_full = jnp.concatenate([queries, other_q], axis=-1)
    fresh_keys_full = jnp.concatenate([fresh_keys, other_k], axis=-1)

    query_all = lax.all_gather(query_full[:, None], "batch", axis=1, tiled=True)

    beam_ids = jnp.broadcast_to(jnp.arange(BEAMS, dtype=jnp.int32)[:, None], (BEAMS, requests))
    choices = jnp.arange(BEAMS, dtype=jnp.int32)[None, :, None]
    new_ok_steps = []
    old_ok_steps = []
    lineage = None
    for step_index in range(steps):
        pick = parents[step_index][:, None, :] == choices
        if lineage is None:
            root = parents[0]
            earlier = None
        else:
            stacked = jnp.concatenate([earlier, root[None]], axis=0)
            moved = jnp.sum(jnp.where(pick[None], stacked[:, None], 0), axis=2)
            earlier, root = moved[:-1], moved[-1]
        own = beam_ids[None]
        earlier = own if earlier is None else jnp.concatenate([earlier, own], axis=0)
        lineage = earlier
        hit = earlier == batch_index
        if step_index + 1 < steps:
            hit = jnp.concatenate(
                [hit, jnp.zeros((steps - 1 - step_index, BEAMS, requests), bool)], axis=0
            )
        new_ok_steps.append(jnp.moveaxis(hit, 0, -1))
        old_ok_steps.append(root == batch_index)
    new_ok = jnp.stack(new_ok_steps, axis=0)
    old_ok = jnp.stack(old_ok_steps, axis=0)

    old_values = old_cache[0, :, 1]
    old_scores = jnp.einsum(
        "sbrc,rhc->sbrh", query_all, old_keys_full, preferred_element_type=jnp.float32
    ) * scale_factor
    new_scores = jnp.einsum(
        "sbrc,trc->sbrt", query_all, fresh_keys_full, preferred_element_type=jnp.float32
    ) * scale_factor

    query_local = lax.dynamic_index_in_dim(
        query_all.reshape(steps, BEAMS, local_reqs, groups, 2 * columns), batch_index, 3, False
    )
    prompt_scores = jnp.einsum(
        "sbrc,rtc->sbrt", query_local, prompt_keys_full, preferred_element_type=jnp.float32
    ) * scale_factor

    old_mask = old_ok[..., None]
    old_masked = jnp.where(old_mask, old_scores, NEG_FILL)
    new_masked = jnp.where(new_ok, new_scores, NEG_FILL)
    chain_peak = jnp.maximum(jnp.max(old_masked, axis=-1), jnp.max(new_masked, axis=-1))
    old_w = jnp.where(old_mask, jnp.exp(old_masked - chain_peak[..., None]), 0.0)
    new_w = jnp.where(new_ok, jnp.exp(new_masked - chain_peak[..., None]), 0.0)
    chain_total = jnp.sum(old_w, axis=-1) + jnp.sum(new_w, axis=-1)
    chain_mix = jnp.einsum(
        "sbrh,rhc->sbrc", old_w.astype(jnp.bfloat16), old_values, preferred_element_type=jnp.float32
    ) + jnp.einsum(
        "sbrt,trc->sbrc",
        new_w.astype(jnp.bfloat16),
        fresh_values,
        preferred_element_type=jnp.float32,
    )

    prompt_mask = (jnp.arange(prompt_span)[None, :] < length_local[:, None])[None, None]
    prompt_masked = jnp.where(prompt_mask, prompt_scores, NEG_FILL)
    prompt_peak = jnp.max(prompt_masked, axis=-1)
    prompt_w = jnp.where(prompt_mask, jnp.exp(prompt_masked - prompt_peak[..., None]), 0.0)
    prompt_total = jnp.sum(prompt_w, axis=-1)
    prompt_mix = jnp.einsum(
        "sbrt,rtc->sbrc",
        prompt_w.astype(jnp.bfloat16),
        prompt_values,
        preferred_element_type=jnp.float32,
    )

    slot_hit = (jnp.arange(groups) == batch_index)[None, None, None, :]
    def spread(values, fill):
        placed = jnp.where(slot_hit, values[..., None], fill)
        return placed.reshape(values.shape[:2] + (requests,))

    def spread_mix(values):
        placed = jnp.where(slot_hit[..., None], values[:, :, :, None, :], 0.0)
        return placed.reshape(values.shape[:2] + (requests, columns))

    p_peak = spread(prompt_peak, NEG_FILL)
    p_total = spread(prompt_total, 0.0)
    p_mix = spread_mix(prompt_mix)
    peak = jnp.maximum(chain_peak, p_peak)
    f_chain = jnp.exp(chain_peak - peak)
    f_prompt = jnp.exp(p_peak - peak)
    total = chain_total * f_chain + p_total * f_prompt
    mix = chain_mix * f_chain[..., None] + p_mix * f_prompt[..., None]

    packed = jnp.concatenate([mix, peak[..., None], total[..., None]], axis=-1)
    received = lax.all_to_all(packed, "batch", 1, 1, tiled=True)
    r_mix = received[..., :columns]
    r_peak = received[..., columns]
    r_total = received[..., columns + 1]
    g_peak = jnp.max(r_peak, axis=1, keepdims=True)
    factor = jnp.exp(r_peak - g_peak)
    all_total = jnp.sum(r_total * factor, axis=1)
    all_mix = jnp.sum(r_mix * factor[..., None], axis=1)
    attention = (all_mix / all_total[..., None]).astype(jnp.bfloat16)

    update = (
        jnp.einsum("src,cd->rsd", attention, out_weight, preferred_element_type=jnp.float32)
        + ffn_update
    )
    summed = jnp.concatenate(
        [
            tree_reduce_scatter(piece, "tensor", order)
            for piece, order in zip(split_last(update, len(SCATTER_ORDERS)), SCATTER_ORDERS)
        ],
        axis=-1,
    )
    result = inputs[:, 0].astype(jnp.float32) + summed[:, None] + down_bias
    return result[:, None]


def solution(mesh):
    in_specs = (
        P(None, "batch", "tensor", None),
        P(),
        P(),
        P(None, None, "tensor"),
        P("tensor", None),
        P(None, "tensor"),
        P("tensor"),
        P("tensor", None),
        P(),
        P("batch", None, None, "tensor"),
        P("batch", None, None, None, "tensor"),
        P(),
        P(),
        P(),
    )
    out_specs = P(None, "batch", "tensor", None)
    return jax.shard_map(
        on_device, mesh=mesh, in_specs=in_specs, out_specs=out_specs, check_vma=False
    )
```
